256 devices in a mesh: dp: 16 (over x, y), mp: 16 (over z, core).
Axes of the slice: x: 4, y: 4, z: 8, core: 2. Of those that a mesh axis runs over, the one named last changes fastest.
Arguments:
- hidden_in: bfloat16 [2, 8192, 2048], P(None, 'dp', 'mp'), may hold values from -6 to 6
- in_gain: float32 [2, 2048], replicated, may hold values from 0.5 to 1.5
- w_zx: bfloat16 [2, 2048, 2, 4096], P(None, None, None, 'mp'), may hold values from -0.125 to 0.125
- w_bc: bfloat16 [2, 2048, 256], replicated, may hold values from -0.125 to 0.125
- w_dt: bfloat16 [2, 2048, 64], P(None, None, 'mp'), may hold values from -0.125 to 0.125
- conv_x: float32 [2, 4, 4096], P(None, None, 'mp'), may hold values from -3 to 3
- conv_bc: float32 [2, 4, 256], replicated, may hold values from -3 to 3
- dt_bias: float32 [2, 64], P(None, 'mp'), may hold values from -1 to 0.5
- a_rate: float32 [2, 64], P(None, 'mp'), may hold values from 2.4414063e-05 to 0.05
- d_skip: float32 [2, 64], P(None, 'mp'), may hold values from 0.5 to 1.5
- gate_gain: float32 [2, 4096], P(None, 'mp'), may hold values from 0.5 to 1.5
- w_out: bfloat16 [2, 4096, 2048], P(None, 'mp'), may hold values from -0.09375 to 0.09375
- final_gain: float32 [2, 2048], replicated, may hold values from 0.5 to 1.5
- lm_head: bfloat16 [2, 26624, 2048], P(None, 'mp', 'dp'), may hold values from -4 to 4
- page_request: int32 [32], replicated, may hold values from 0 to 7, never falling along the last dimension, each value on 1 to 16 neighbouring positions
- targets: int32 [8192], P('dp'), may hold values from 0 to 26623
- owners: int32 [8], replicated, may hold values from 0 to 15
Outputs:
- token_ratio: float32 [8192], P('dp')
- owned: float32 [16, 8], P('dp')
The draws below stay inside these ranges and needn't reach their ends.
Inputs may be any that keep to these rules, and one draw needn't show every extreme that they name: page_request[k] is the request of page k; the pages of a request are consecutive and requests appear in increasing order; every request has 1 to 16 pages, and one has exactly 16. owners[r] is the dp index that receives request r's mean; several requests may share an owner.
All inputs are finite; a program needn't handle non-finite values.
Results may differ from the reference program's by a relative error of at most 0.0085.
Values may be sent and summed in bfloat16 or wider, within the bound.
No kernel may reach another device: no remote copies, remote signals or barrier semaphores. Data moves between devices by JAX's collectives and lax.ppermute only.
A program may use at most 128 MiB of HBM per device.

```python
import math
import jax
import jax.numpy as jnp
import numpy as np
from jax import lax

D = 2048
INNER = 4096
HEADS = 64
HEADDIM = 64
STATE = 128
CONV = 4
VOCAB = 26624
PAGE = 256
PAGES = 32
TOKENS = 8192
REQ = 8
MOST_PAGES = 16
N_DP = 16


def shared_sign(key):
    flips = jax.random.bernoulli(jax.random.fold_in(key, 77), 0.5, (D,))
    return jnp.where(flips, 1.0, -1.0).astype(jnp.float32)


def draw_hidden_in(key, part):
    first_key, second_key, third_key = jax.random.split(jax.random.fold_in(key, 21), 3)
    base = jax.random.normal(first_key, (2, TOKENS, D), jnp.float32)
    base = jnp.clip(base, -6.0, 6.0)
    offset = jax.random.randint(second_key, (), 0, 32)
    positions = jnp.arange(TOKENS)
    chosen = (positions + offset) % 32 == 0
    strength = jax.random.uniform(third_key, (2, TOKENS, 1), jnp.float32, 2.0, 5.0)
    signs = shared_sign(key)
    spiked = jnp.clip(strength * signs[None, None, :] + 0.3 * base, -6.0, 6.0)
    return jnp.where(chosen[None, :, None], spiked, base).astype(jnp.bfloat16)


def draw_lm_head(key, part):
    first_key = jax.random.fold_in(jax.random.fold_in(key, 11), 0)
    entries = jnp.clip(jax.random.normal(first_key, (2, VOCAB, D), jnp.float32), -4.0, 4.0)
    entries = entries / math.sqrt(D)
    first_row = jax.random.randint(jax.random.fold_in(key, 31), (), 0, VOCAB // 2)
    signs = shared_sign(key)
    vocab_rows = jnp.arange(VOCAB)[None, :, None]
    strong = 250.0 / D * signs[None, None, :]
    entries = jnp.where(vocab_rows == first_row, strong, entries)
    entries = jnp.where(vocab_rows == first_row + VOCAB // 2, 0.99 * strong, entries)
    return entries.astype(jnp.bfloat16)


def place_ends(values, rng, least, top_value):
    longest = values.shape.index(max(values.shape))
    spots = []
    for shift in (0, 1):
        where = [jax.random.randint(jax.random.fold_in(rng, axis), (), 0, length) for axis, length in enumerate(values.shape)]
        where[longest] = (where[longest] + shift) % values.shape[longest]
        spots.append(tuple(where))
    return values.at[spots[0]].set(least).at[spots[1]].set(top_value)


def shard_levels(own_key, shape, pieces, low, high):
    def one(position, shards_of):
        steps = jax.random.uniform(jax.random.fold_in(jax.random.fold_in(own_key, 6), position), (shards_of,), jnp.float32, low / len(pieces), high / len(pieces))
        return jnp.repeat(jnp.exp(steps), shape[position] // shards_of).reshape((-1,) + (1,) * (len(shape) - position - 1))

    level = one(*pieces[0])
    for cut in pieces[1:]:
        level = level * one(*cut)
    return level


def cumulative_ranks(number_of, lean):
    loads = [(1 << 20) // math.isqrt(grade ** lean) + 1 for grade in range(1, number_of + 1)]
    scale = 1 + sum(loads) // (1 << 30)
    return np.cumsum(np.array([max(1, weight // scale) for weight in loads]))


def ranked_ids(key, dims, count, skew):
    grid = cumulative_ranks(count, skew)
    pick = jax.random.randint(jax.random.fold_in(key, 1), dims, 0, int(grid[count - 1]))
    grade = jnp.searchsorted(jnp.asarray(grid, jnp.int32), pick, side="right")
    return jax.random.permutation(jax.random.fold_in(key, 2), count)[grade].astype(jnp.int32)


def length_profile(count, total, limit, skew):
    portions = [(1 << 20) // math.isqrt(grade ** skew) + 1 for grade in range(2, count + 1)]
    rest, given = total - limit - (count - 1), [1] * (count - 1)
    while rest > 0:
        movable = [i for i in range(count - 1) if given[i] < limit]
        mass, remaining = sum([portions[i] for i in movable]), rest
        for i in movable:
            more = min(limit - given[i], max(1, remaining * portions[i] // mass), rest)
            given[i] = given[i] + more
            rest = rest - more
    return np.array([limit] + given)


def ragged_sizes(own_key, count, total, bound, slope):
    if count == 2:
        one = jax.random.randint(own_key, (), max(1, total - bound), min(bound, total - 1) + 1)
        return jnp.stack([one, total - one])
    sizes = jnp.asarray(length_profile(count, total, bound, slope), jnp.int32)
    pairs = (count - 1) // 2
    giver, sink = sizes[1:1 + 2 * pairs:2], sizes[2:2 + 2 * pairs:2]
    slack = jnp.minimum(giver - 1, bound - sink)
    passed = jax.random.randint(jax.random.fold_in(own_key, 1), (pairs,), 0, 1 << 20) % (slack + 1)
    sizes = sizes.at[1:1 + 2 * pairs:2].set(giver - passed).at[2:2 + 2 * pairs:2].set(sink + passed)
    return sizes[jax.random.permutation(jax.random.fold_in(own_key, 2), count)]


def bell_draw(rng, shape, scale, most, shards=(), kind=jnp.bfloat16):
    values = jax.random.normal(rng, shape, jnp.float32) * scale
    if len(shards) > 0:
        values = shard_levels(rng, shape, shards, -0.22, 0.18) * values
    return jnp.clip(values, min=-most, max=most).astype(kind)


def setup_inputs(seed: int = 0) -> dict:
    splits = jax.random.split(jax.random.key(seed), 18)
    return {
        "hidden_in": draw_hidden_in(jax.random.fold_in(splits[17], 71), 0),
        "in_gain": jnp.clip(1.0 + 0.1 * jax.random.normal(splits[1], (2, D), jnp.float32), 0.5, 1.5),
        "w_zx": bell_draw(splits[2], (2, D, 2, INNER), D ** -0.5, 0.125, ((3, 16),)),
        "w_bc": bell_draw(splits[3], (2, D, 2 * STATE), D ** -0.5, 0.125),
        "w_dt": bell_draw(splits[4], (2, D, HEADS), D ** -0.5, 0.125, ((2, 16),)),
        "conv_x": bell_draw(splits[5], (2, CONV, INNER), 0.5, 3.0, ((2, 16),), jnp.float32),
        "conv_bc": bell_draw(splits[6], (2, CONV, 2 * STATE), 0.5, 3.0, (), jnp.float32),
        "dt_bias": jnp.clip(-1.0 + 1.5 * jax.random.uniform(splits[7], (2, HEADS), jnp.float32) ** shard_levels(splits[7], (2, HEADS), ((1, 16),), -0.2, 0.2), -1.0, 0.5),
        "a_rate": jnp.clip(jnp.exp(math.log(0.05) - 7.624619 * jax.random.uniform(splits[8], (2, HEADS), jnp.float32) ** shard_levels(splits[8], (2, HEADS), ((1, 16),), -0.2, 0.2)), 2.441406286379788e-05, 0.05),
        "d_skip": jnp.clip(0.5 + 1.0 * jax.random.uniform(splits[9], (2, HEADS), jnp.float32) ** shard_levels(splits[9], (2, HEADS), ((1, 16),), -0.2, 0.2), 0.5, 1.5),
        "gate_gain": jnp.clip(1.0 + 0.1 * jax.random.normal(splits[10], (2, INNER), jnp.float32), 0.5, 1.5),
        "w_out": bell_draw(splits[11], (2, INNER, D), INNER ** -0.5, 0.09375, ((1, 16),)),
        "final_gain": jnp.clip(1.0 + 0.1 * jax.random.normal(splits[12], (2, D), jnp.float32), 0.5, 1.5),
        "lm_head": draw_lm_head(jax.random.fold_in(splits[17], 71), 0),
        "page_request": jnp.searchsorted(jnp.cumsum(ragged_sizes(splits[14], REQ, PAGES, MOST_PAGES, 2)), jnp.arange(PAGES), side="right").astype(jnp.int32),
        "targets": place_ends(ranked_ids(splits[15], (TOKENS,), VOCAB, 2), jax.random.fold_in(splits[15], 3), 0, VOCAB - 1).astype(jnp.int32),
        "owners": place_ends(jax.random.randint(splits[16], (REQ,), 0, N_DP), jax.random.fold_in(splits[16], 1), 0, N_DP - 1).astype(jnp.int32),
    }


EPS = 1e-05
HIGH = lax.Precision.HIGHEST

def rms_scale(rows, gain):
    mean_square = lax.optimization_barrier(jnp.mean(rows * rows, axis=-1, keepdims=True))
    return rows * lax.rsqrt(mean_square + EPS) * gain

def page_starts(page_request):
    previous = jnp.concatenate([jnp.full((1,), -1, jnp.int32), page_request[:-1].astype(jnp.int32)])
    return page_request.astype(jnp.int32) != previous

def causal_conv(inputs, weights, token_req):
    width = weights.shape[0]
    wide = inputs.astype(jnp.float32)
    total = wide * weights[width - 1]
    for back in range(1, width):
        shifted = jnp.concatenate([jnp.zeros((back, wide.shape[1]), jnp.float32), wide[:-back]], axis=0)
        same_req = jnp.concatenate([jnp.zeros((back,), bool), token_req[back:] == token_req[:-back]])
        total = total + jnp.where(same_req[:, None], shifted, 0.0) * weights[width - 1 - back]
    return jax.nn.silu(total).astype(jnp.bfloat16)

def page_output(c_page, b_page, x_page, dt_page, la_page, state_in, skip):
    length = c_page.shape[0]
    cum = jnp.cumsum(la_page, axis=0)
    inner = jnp.einsum('ln,sn->ls', c_page, b_page, precision=HIGH)
    rows = jnp.arange(length)
    lower = (rows[:, None] >= rows[None, :])[:, :, None]
    spread = cum[:, None, :] - cum[None, :, :]
    decay = jnp.where(lower, jnp.exp(jnp.where(lower, spread, 0.0)), 0.0)
    mixing = inner[:, :, None] * decay * dt_page[None, :, :]
    y_intra = jnp.einsum('lsh,shp->lhp', mixing, x_page, precision=HIGH)
    y_carry = jnp.exp(cum)[:, :, None] * jnp.einsum('ln,hpn->lhp', c_page, state_in, precision=HIGH)
    tail = jnp.exp(cum[-1][None, :] - cum) * dt_page
    page_end = jnp.einsum('sh,shp,sn->hpn', tail, x_page, b_page, precision=HIGH)
    return (y_intra + y_carry + skip[None, :, None] * x_page, page_end, jnp.exp(cum[-1]))

def one_model(hidden, in_gain, w_zx, w_bc, w_dt, conv_x, conv_bc, dt_bias, a_rate, d_skip, gate_gain, w_out, final_gain, lm_head, page_request, targets):
    token_req = jnp.repeat(page_request.astype(jnp.int32), PAGE)
    wide_in = hidden.astype(jnp.float32)
    normed = rms_scale(wide_in, in_gain).astype(jnp.bfloat16)
    gate = jnp.dot(normed, w_zx[:, 0, :], preferred_element_type=jnp.float32).astype(jnp.bfloat16)
    values = jnp.dot(normed, w_zx[:, 1, :], preferred_element_type=jnp.float32).astype(jnp.bfloat16)
    proj_bc = jnp.dot(normed, w_bc, preferred_element_type=jnp.float32).astype(jnp.bfloat16)
    proj_dt = jnp.dot(normed, w_dt, preferred_element_type=jnp.float32).astype(jnp.bfloat16)
    conv_values = causal_conv(values, conv_x, token_req)
    conv_b_c = causal_conv(proj_bc, conv_bc, token_req)
    step_size = jax.nn.softplus(proj_dt.astype(jnp.float32) + dt_bias)
    log_decay = -step_size * a_rate
    starts = page_starts(page_request)
    x_pages = conv_values.astype(jnp.float32).reshape(PAGES, PAGE, HEADS, HEADDIM)
    b_pages = conv_b_c[:, :STATE].astype(jnp.float32).reshape(PAGES, PAGE, STATE)
    c_pages = conv_b_c[:, STATE:].astype(jnp.float32).reshape(PAGES, PAGE, STATE)
    dt_pages = step_size.reshape(PAGES, PAGE, HEADS)
    la_pages = log_decay.reshape(PAGES, PAGE, HEADS)

    def advance(state, page):
        start_flag, c_page, b_page, x_page, dt_page, la_page = page
        state_in = jnp.where(start_flag, jnp.float32(0.0), state)
        result, page_end, page_decay = page_output(c_page, b_page, x_page, dt_page, la_page, state_in, d_skip)
        return (page_decay[:, None, None] * state_in + page_end, result)
    initial = jnp.zeros((HEADS, HEADDIM, STATE), jnp.float32)
    _, scanned = lax.scan(advance, initial, (starts, c_pages, b_pages, x_pages, dt_pages, la_pages))
    gated = scanned.reshape(TOKENS, INNER) * jax.nn.silu(gate.astype(jnp.float32))
    mixer_out = rms_scale(gated, gate_gain).astype(jnp.bfloat16)
    resid = wide_in + jnp.dot(mixer_out, w_out, preferred_element_type=jnp.float32)
    final = rms_scale(resid, final_gain).astype(jnp.bfloat16)

    def block_logprob(block):
        rows_in, ids = block
        logits = jnp.dot(rows_in, lm_head.T, preferred_element_type=jnp.float32)
        top = lax.optimization_barrier(jnp.max(logits, axis=1))
        total = lax.optimization_barrier(jnp.sum(jnp.exp(logits - top[:, None]), axis=1))
        picked = jnp.take_along_axis(logits, ids[:, None].astype(jnp.int32), axis=1)[:, 0]
        return picked - (top + jnp.log(total))
    logprob = lax.map(block_logprob, (final.reshape(PAGES, PAGE, D), targets.reshape(PAGES, PAGE)))
    return logprob.reshape(TOKENS)

def reference(hidden_in, in_gain, w_zx, w_bc, w_dt, conv_x, conv_bc, dt_bias, a_rate, d_skip, gate_gain, w_out, final_gain, lm_head, page_request, targets, owners):
    results = []
    for model in range(2):
        results.append(one_model(hidden_in[model], in_gain[model], w_zx[model], w_bc[model], w_dt[model], conv_x[model], conv_bc[model], dt_bias[model], a_rate[model], d_skip[model], gate_gain[model], w_out[model], final_gain[model], lm_head[model], page_request, targets))
    token_ratio = results[0] - results[1]
    page_sums = lax.optimization_barrier(jnp.sum(token_ratio.reshape(PAGES, PAGE), axis=1))
    onehot = (page_request[:, None].astype(jnp.int32) == jnp.arange(REQ, dtype=jnp.int32)[None, :]).astype(jnp.float32)
    counts = lax.optimization_barrier(jnp.sum(onehot, axis=0)) * PAGE
    seq_mean = lax.optimization_barrier(jnp.sum(page_sums[:, None] * onehot, axis=0)) / counts
    owner_mask = owners[None, :].astype(jnp.int32) == jnp.arange(N_DP, dtype=jnp.int32)[:, None]
    owned = jnp.where(owner_mask, seq_mean[None, :], jnp.float32(0.0))
    return (token_ratio, owned)
```

```python
import jax
import jax.numpy as jnp
from jax import lax
from jax.sharding import PartitionSpec as P

D = 2048
INNER = 4096
HEADDIM = 64
STATE = 128
PAGE = 256
MOST_PAGES = 16


EPS = 1e-05
HIGH = lax.Precision.HIGHEST


def shifted(block, axis, distance):
    devices = range(lax.axis_size(axis))
    route = [(i - distance, i) for i in devices if i - distance in devices]
    return lax.ppermute(block, axis, route)


def entering(shard, axis, combine, identity):
    peers, index = (lax.axis_size(axis), lax.axis_index(axis))
    everything = jax.tree.map(lambda part: lax.all_gather(part, axis), shard)
    start = jax.tree.map(
        lambda part, zero: jnp.broadcast_to(jnp.asarray(zero, part.dtype), part.shape),
        shard,
        identity,
    )

    def turn(k, before):
        reached = k < index
        new = combine(before, jax.tree.map(lambda part: part[k], everything))
        return jax.tree.map(lambda a, b: jnp.where(reached, a, b), new, before)

    return lax.fori_loop(0, peers, turn, start)


def fan_out(block, axis, shifts):
    devices = lax.axis_size(axis)
    return [
        lax.ppermute(block, axis, [(i, (i + s) % devices) for i in range(devices)]) for s in shifts
    ]


def rms_scale(rows, gain):
    mean_square = jnp.mean(rows * rows, axis=-1, keepdims=True)
    return rows * lax.rsqrt(mean_square + EPS) * gain


def page_conv(current, previous, weights):
    width = weights.shape[1]
    length = current.shape[2]
    padded = jnp.concatenate([previous, current], axis=2).astype(jnp.float32)
    total = padded[:, :, width - 1 : width - 1 + length, :] * weights[:, None, None, width - 1, :]
    for back in range(1, width):
        begin = width - 1 - back
        total = (
            total
            + padded[:, :, begin : begin + length, :] * weights[:, None, None, width - 1 - back, :]
        )
    return jax.nn.silu(total).astype(jnp.bfloat16)


def link_states(earlier, later):
    later_flag = later[0]
    keep = 1.0 - later_flag
    return (
        jnp.maximum(earlier[0], later_flag),
        later[1] * (later_flag + keep * earlier[1]),
        later[2] + keep * later[1][..., None, None] * earlier[2],
    )


def local(
    hidden_in,
    in_gain,
    w_zx,
    w_bc,
    w_dt,
    conv_x,
    conv_bc,
    dt_bias,
    a_rate,
    d_skip,
    gate_gain,
    w_out,
    final_gain,
    lm_head,
    page_request,
    targets,
    owners,
):
    n_dp = lax.axis_size("dp")
    dp_index = lax.axis_index("dp")
    mp_index = lax.axis_index("mp")
    tokens = hidden_in.shape[1]
    num_pages = tokens // PAGE
    local_inner = w_zx.shape[3]
    local_heads = w_dt.shape[2]
    width = conv_x.shape[1]
    all_starts = page_request != jnp.concatenate([jnp.full((1,), -1, jnp.int32), page_request[:-1]])
    my_starts = lax.dynamic_slice_in_dim(all_starts, dp_index * num_pages, num_pages)
    my_req = lax.dynamic_slice_in_dim(page_request, dp_index * num_pages, num_pages)
    page_flags = my_starts.astype(jnp.float32)
    full_in = lax.all_gather(hidden_in, "mp", axis=2, tiled=True)
    head_in, full_in = lax.optimization_barrier((lm_head, full_in))
    wide_in = full_in.astype(jnp.float32)
    normed = rms_scale(wide_in, in_gain[:, None, :]).astype(jnp.bfloat16)
    zx_cols = w_zx.reshape(2, D, 2 * local_inner)
    proj_zx = jnp.einsum(
        "mtd,mde->mte", normed, zx_cols, preferred_element_type=jnp.float32
    ).astype(jnp.bfloat16)
    gate = proj_zx[:, :, :local_inner]
    values = proj_zx[:, :, local_inner:]
    proj_bc = jnp.einsum("mtd,mde->mte", normed, w_bc, preferred_element_type=jnp.float32).astype(
        jnp.bfloat16
    )
    proj_dt = jnp.einsum("mtd,mde->mte", normed, w_dt, preferred_element_type=jnp.float32).astype(
        jnp.bfloat16
    )
    rim_x, rim_bc = shifted(
        (values[:, tokens - (width - 1) :, :], proj_bc[:, tokens - (width - 1) :, :]), "dp", 1
    )
    value_pages = values.reshape(2, num_pages, PAGE, local_inner)
    bc_pages = proj_bc.reshape(2, num_pages, PAGE, 2 * STATE)
    cut_mask = my_starts[None, :, None, None]
    prev_x = jnp.concatenate([rim_x[:, None], value_pages[:, :-1, PAGE - (width - 1) :, :]], axis=1)
    prev_x = jnp.where(cut_mask, jnp.zeros_like(prev_x), prev_x)
    prev_bc = jnp.concatenate([rim_bc[:, None], bc_pages[:, :-1, PAGE - (width - 1) :, :]], axis=1)
    prev_bc = jnp.where(cut_mask, jnp.zeros_like(prev_bc), prev_bc)
    conv_values = page_conv(value_pages, prev_x, conv_x)
    conv_b_c = page_conv(bc_pages, prev_bc, conv_bc)
    step_size = jax.nn.softplus(proj_dt.astype(jnp.float32) + dt_bias[:, None, :])
    log_decay = -step_size * a_rate[:, None, :]
    x_pages = conv_values.astype(jnp.float32).reshape(2, num_pages, PAGE, local_heads, HEADDIM)
    b_pages = conv_b_c[..., :STATE].astype(jnp.float32)
    c_pages = conv_b_c[..., STATE:].astype(jnp.float32)
    dt_pages = step_size.reshape(2, num_pages, PAGE, local_heads)
    cum = jnp.cumsum(log_decay.reshape(2, num_pages, PAGE, local_heads), axis=2)
    inner = jnp.einsum("mkln,mksn->mkls", c_pages, b_pages, precision=HIGH)
    rows = jnp.arange(PAGE)
    lower = (rows[:, None] >= rows[None, :])[None, None, :, :, None]
    spread = cum[:, :, :, None, :] - cum[:, :, None, :, :]
    decay = jnp.where(lower, jnp.exp(jnp.where(lower, spread, 0.0)), 0.0)
    mixing = inner[..., None] * decay * dt_pages[:, :, None, :, :]
    y_intra = jnp.einsum("mklsh,mkshp->mklhp", mixing, x_pages, precision=HIGH)
    tail = jnp.exp(cum[:, :, -1:, :] - cum) * dt_pages
    page_end = jnp.einsum("mksh,mkshp,mksn->mkhpn", tail, x_pages, b_pages, precision=HIGH)
    page_decay = jnp.exp(cum[:, :, -1, :])
    summary = (
        jnp.zeros((1,), jnp.float32),
        jnp.ones((2, local_heads), jnp.float32),
        jnp.zeros((2, local_heads, HEADDIM, STATE), jnp.float32),
    )
    for page in range(num_pages):
        summary = link_states(
            summary, (page_flags[page : page + 1], page_decay[:, page], page_end[:, page])
        )
    gate_through = summary[1] * (1.0 - summary[0])
    lane = jnp.arange(STATE)[None, None, None, :] == 0
    packed = jnp.concatenate(
        [summary[2], jnp.where(lane, gate_through[..., None, None], 0.0)], axis=2
    )
    reach = min(n_dp - 1, (MOST_PAGES * PAGE) // tokens)
    carried = jnp.zeros_like(summary[2])
    weight = jnp.ones_like(gate_through)
    for s in range(1, reach + 1):
        got = lax.ppermute(packed, "dp", [(i, i + s) for i in range(n_dp - s)])
        valid = (dp_index >= s).astype(jnp.float32)
        carried = carried + (valid * weight)[..., None, None] * got[:, :, :HEADDIM, :]
        weight = weight * got[:, :, HEADDIM, 0]
    state_in = (1.0 - page_flags[0]) * carried
    outputs = []
    for page in range(num_pages):
        if page > 0:
            state_in = (1.0 - page_flags[page]) * (
                page_decay[:, page - 1][..., None, None] * state_in + page_end[:, page - 1]
            )
        y_carry = jnp.exp(cum[:, page])[..., None] * jnp.einsum(
            "mln,mhpn->mlhp", c_pages[:, page], state_in, precision=HIGH
        )
        outputs.append(y_intra[:, page] + y_carry + d_skip[:, None, :, None] * x_pages[:, page])
    scanned = jnp.stack(outputs, axis=1).reshape(2, tokens, local_inner)
    gated = scanned * jax.nn.silu(gate.astype(jnp.float32))
    gate_squares = jnp.sum(gated * gated, axis=2)
    unscaled = (gated * gate_gain[:, None, :]).astype(jnp.bfloat16)
    partial_out = jnp.einsum("mti,mid->mtd", unscaled, w_out, preferred_element_type=jnp.float32)
    extra = jnp.where(
        jnp.arange(128)[None, None, :] == 0, gate_squares[..., None], 0.0
    )
    head_all = lax.all_gather(head_in, "dp", axis=2, tiled=True)
    ready, head_all = lax.optimization_barrier((jnp.concatenate([partial_out, extra], axis=2), head_all))
    summed = lax.psum_scatter(ready, "mp", scatter_dimension=1, tiled=True)
    rows_here = summed.shape[1]
    gate_total = summed[:, :, D]
    mixed = summed[:, :, :D] * lax.rsqrt(gate_total[..., None] / INNER + EPS)
    mine = lax.dynamic_slice_in_dim(wide_in, mp_index * rows_here, rows_here, axis=1)
    final_part = rms_scale(mine + mixed, final_gain[:, None, :]).astype(jnp.bfloat16)
    final = lax.all_gather(final_part, "mp", axis=1, tiled=True)
    vocab_local = lm_head.shape[1]
    logits = jnp.einsum(
        "mtd,mvd->mtv",
        final,
        head_all,
        preferred_element_type=jnp.float32,
    )
    top_here = jnp.max(logits, axis=2)
    exp_here = jnp.sum(jnp.exp(logits - top_here[..., None]), axis=2)
    local_ids = targets - mp_index * vocab_local
    hit = jnp.arange(vocab_local, dtype=jnp.int32)[None, None, :] == local_ids[None, :, None]
    picked_here = jnp.sum(jnp.where(hit, logits, 0.0), axis=2)
    here = jnp.stack([top_here, exp_here, picked_here])
    stats = jnp.stack([here] + fan_out(here, "mp", range(1, lax.axis_size("mp"))))
    top = jnp.max(stats[:, 0], axis=0)
    exp_total = jnp.sum(stats[:, 1] * jnp.exp(stats[:, 0] - top[None]), axis=0)
    picked = jnp.sum(stats[:, 2], axis=0)
    logprob = picked - (top + jnp.log(exp_total))
    token_ratio = logprob[0] - logprob[1]
    request_count = owners.shape[0]
    page_sums = jnp.sum(token_ratio.reshape(num_pages, PAGE), axis=1)
    request_ids = jnp.arange(request_count, dtype=jnp.int32)
    all_onehot = (page_request[:, None] == request_ids[None, :]).astype(jnp.float32)
    counts = jnp.sum(all_onehot, axis=0) * PAGE
    my_onehot = (my_req[:, None] == request_ids[None, :]).astype(jnp.float32)
    partial_mean = jnp.sum(page_sums[:, None] * my_onehot, axis=0) / counts
    seq_mean = sum(fan_out(partial_mean, "dp", range(1, n_dp)), partial_mean)
    owned = jnp.where(owners == dp_index, seq_mean, jnp.float32(0.0))[None, :]
    return (token_ratio, owned)


def solution(mesh):
    placed = (
        P(None, "dp", "mp"),
        P(),
        P(None, None, None, "mp"),
        P(),
        P(None, None, "mp"),
        P(None, None, "mp"),
        P(),
        P(None, "mp"),
        P(None, "mp"),
        P(None, "mp"),
        P(None, "mp"),
        P(None, "mp", None),
        P(),
        P(None, "mp", "dp"),
        P(),
        P("dp"),
        P(),
    )
    return jax.shard_map(
        local, mesh=mesh, in_specs=placed, out_specs=(P("dp"), P("dp", None)), check_vma=False
    )
```

```python
import jax
import jax.numpy as jnp
from jax import lax
from jax.sharding import PartitionSpec as P

D = 2048
INNER = 4096
HEADDIM = 64
STATE = 128
PAGE = 256


EPS = 1e-05
HIGH = lax.Precision.HIGHEST


def shifted(block, axis, distance):
    devices = range(lax.axis_size(axis))
    route = [(i - distance, i) for i in devices if i - distance in devices]
    return lax.ppermute(block, axis, route)


def entering(shard, axis, combine, identity):
    peers, index = (lax.axis_size(axis), lax.axis_index(axis))
    everything = jax.tree.map(lambda part: lax.all_gather(part, axis), shard)
    start = jax.tree.map(
        lambda part, zero: jnp.broadcast_to(jnp.asarray(zero, part.dtype), part.shape),
        shard,
        identity,
    )

    def turn(k, before):
        reached = k < index
        new = combine(before, jax.tree.map(lambda part: part[k], everything))
        return jax.tree.map(lambda a, b: jnp.where(reached, a, b), new, before)

    return lax.fori_loop(0, peers, turn, start)


def torus_gather(shard, axis, rows, cols, row_first):
    index = lax.axis_index(axis)
    row, col = (index // cols, index % cols)

    def step(block, along_rows, shifts):
        moved = [block]
        for s in shifts:
            if along_rows:
                route = [(r * cols + c, ((r + s) % rows) * cols + c) for r in range(rows) for c in range(cols)]
            else:
                route = [(r * cols + c, r * cols + (c + s) % cols) for r in range(rows) for c in range(cols)]
            moved.append(lax.ppermute(block, axis, route))
        return jnp.stack(moved)

    if row_first:
        sources = [((row - a) % rows) * cols + (col - b) % cols for b in range(cols) for a in range(rows)]
    else:
        sources = [((row - a) % rows) * cols + (col - b) % cols for a in range(rows) for b in range(cols)]

    def second(first):
        both = step(first, not row_first, range(1, cols if row_first else rows))
        return both.reshape((rows * cols,) + shard.shape)

    return step(shard, row_first, range(1, rows if row_first else cols)), second, sources


def rms_scale(rows, gain):
    mean_square = jnp.mean(rows * rows, axis=-1, keepdims=True)
    return rows * lax.rsqrt(mean_square + EPS) * gain


def page_conv(current, previous, weights):
    width = weights.shape[1]
    length = current.shape[2]
    padded = jnp.concatenate([previous, current], axis=2).astype(jnp.float32)
    total = padded[:, :, width - 1 : width - 1 + length, :] * weights[:, None, None, width - 1, :]
    for back in range(1, width):
        begin = width - 1 - back
        total = (
            total
            + padded[:, :, begin : begin + length, :] * weights[:, None, None, width - 1 - back, :]
        )
    return jax.nn.silu(total).astype(jnp.bfloat16)


def link_states(earlier, later):
    later_flag = later[0]
    keep = 1.0 - later_flag
    return (
        jnp.maximum(earlier[0], later_flag),
        later[1] * (later_flag + keep * earlier[1]),
        later[2] + keep * later[1][..., None, None] * earlier[2],
    )


def local(
    hidden_in,
    in_gain,
    w_zx,
    w_bc,
    w_dt,
    conv_x,
    conv_bc,
    dt_bias,
    a_rate,
    d_skip,
    gate_gain,
    w_out,
    final_gain,
    lm_head,
    page_request,
    targets,
    owners,
):
    n_dp = lax.axis_size("dp")
    dp_index = lax.axis_index("dp")
    mp_index = lax.axis_index("mp")
    tokens = hidden_in.shape[1]
    num_pages = tokens // PAGE
    local_inner = w_zx.shape[3]
    local_heads = w_dt.shape[2]
    width = conv_x.shape[1]
    all_starts = page_request != jnp.concatenate([jnp.full((1,), -1, jnp.int32), page_request[:-1]])
    my_starts = lax.dynamic_slice_in_dim(all_starts, dp_index * num_pages, num_pages)
    my_req = lax.dynamic_slice_in_dim(page_request, dp_index * num_pages, num_pages)
    page_flags = my_starts.astype(jnp.float32)
    full_in = lax.all_gather(hidden_in, "mp", axis=2, tiled=True)
    wide_in = full_in.astype(jnp.float32)
    normed = rms_scale(wide_in, in_gain[:, None, :]).astype(jnp.bfloat16)
    zx_cols = w_zx.reshape(2, D, 2 * local_inner)
    proj_zx = jnp.einsum(
        "mtd,mde->mte", normed, zx_cols, preferred_element_type=jnp.float32
    ).astype(jnp.bfloat16)
    gate = proj_zx[:, :, :local_inner]
    values = proj_zx[:, :, local_inner:]
    proj_bc = jnp.einsum("mtd,mde->mte", normed, w_bc, preferred_element_type=jnp.float32).astype(
        jnp.bfloat16
    )
    proj_dt = jnp.einsum("mtd,mde->mte", normed, w_dt, preferred_element_type=jnp.float32).astype(
        jnp.bfloat16
    )
    rim_x, rim_bc = shifted(
        (values[:, tokens - (width - 1) :, :], proj_bc[:, tokens - (width - 1) :, :]), "dp", 1
    )
    value_pages = values.reshape(2, num_pages, PAGE, local_inner)
    bc_pages = proj_bc.reshape(2, num_pages, PAGE, 2 * STATE)
    cut_mask = my_starts[None, :, None, None]
    prev_x = jnp.concatenate([rim_x[:, None], value_pages[:, :-1, PAGE - (width - 1) :, :]], axis=1)
    prev_x = jnp.where(cut_mask, jnp.zeros_like(prev_x), prev_x)
    prev_bc = jnp.concatenate([rim_bc[:, None], bc_pages[:, :-1, PAGE - (width - 1) :, :]], axis=1)
    prev_bc = jnp.where(cut_mask, jnp.zeros_like(prev_bc), prev_bc)
    conv_values = page_conv(value_pages, prev_x, conv_x)
    conv_b_c = page_conv(bc_pages, prev_bc, conv_bc)
    step_size = jax.nn.softplus(proj_dt.astype(jnp.float32) + dt_bias[:, None, :])
    log_decay = -step_size * a_rate[:, None, :]
    x_pages = conv_values.astype(jnp.float32).reshape(2, num_pages, PAGE, local_heads, HEADDIM)
    b_pages = conv_b_c[..., :STATE].astype(jnp.float32)
    c_pages = conv_b_c[..., STATE:].astype(jnp.float32)
    dt_pages = step_size.reshape(2, num_pages, PAGE, local_heads)
    cum = jnp.cumsum(log_decay.reshape(2, num_pages, PAGE, local_heads), axis=2)
    inner = jnp.einsum("mkln,mksn->mkls", c_pages, b_pages, precision=HIGH)
    rows = jnp.arange(PAGE)
    lower = (rows[:, None] >= rows[None, :])[None, None, :, :, None]
    spread = cum[:, :, :, None, :] - cum[:, :, None, :, :]
    decay = jnp.where(lower, jnp.exp(jnp.where(lower, spread, 0.0)), 0.0)
    mixing = inner[..., None] * decay * dt_pages[:, :, None, :, :]
    y_intra = jnp.einsum("mklsh,mkshp->mklhp", mixing, x_pages, precision=HIGH)
    tail = jnp.exp(cum[:, :, -1:, :] - cum) * dt_pages
    page_end = jnp.einsum("mksh,mkshp,mksn->mkhpn", tail, x_pages, b_pages, precision=HIGH)
    page_decay = jnp.exp(cum[:, :, -1, :])
    summary = (
        jnp.zeros((1,), jnp.float32),
        jnp.ones((2, local_heads), jnp.float32),
        jnp.zeros((2, local_heads, HEADDIM, STATE), jnp.float32),
    )
    for page in range(num_pages):
        summary = link_states(
            summary, (page_flags[page : page + 1], page_decay[:, page], page_end[:, page])
        )
    gate_through = summary[1] * (1.0 - summary[0])
    lane = jnp.arange(STATE)[None, None, None, :] == 0
    packed = jnp.concatenate(
        [summary[2], jnp.where(lane, gate_through[..., None, None], 0.0)], axis=2
    )
    vocab_local = lm_head.shape[1]
    half = vocab_local // 2
    feat = lm_head.shape[2]
    staged = [
        torus_gather(part, "dp", 4, n_dp // 4, row_first)
        for row_first, part in ((False, lm_head[:, :half]), (True, lm_head[:, half:]))
    ]
    firsts, packed = lax.optimization_barrier(([s[0] for s in staged], packed))
    every = lax.all_gather(packed, "dp")
    ends = every[:, :, :, :HEADDIM, :]
    through = every[:, :, :, HEADDIM, 0]
    peers = jnp.arange(n_dp)
    factor = jnp.where((peers < dp_index)[:, None, None], through, 1.0)
    weight = jnp.flip(jnp.cumprod(jnp.flip(factor, 0), axis=0), 0)
    weight = jnp.concatenate([weight[1:], jnp.ones_like(weight[:1])], axis=0)
    weight = jnp.where((peers < dp_index)[:, None, None], weight, 0.0)
    carried = jnp.sum(weight[..., None, None] * ends, axis=0)
    state_in = (1.0 - page_flags[0]) * carried
    outputs = []
    for page in range(num_pages):
        if page > 0:
            state_in = (1.0 - page_flags[page]) * (
                page_decay[:, page - 1][..., None, None] * state_in + page_end[:, page - 1]
            )
        y_carry = jnp.exp(cum[:, page])[..., None] * jnp.einsum(
            "mln,mhpn->mlhp", c_pages[:, page], state_in, precision=HIGH
        )
        outputs.append(y_intra[:, page] + y_carry + d_skip[:, None, :, None] * x_pages[:, page])
    scanned = jnp.stack(outputs, axis=1).reshape(2, tokens, local_inner)
    gated = scanned * jax.nn.silu(gate.astype(jnp.float32))
    gate_squares = jnp.sum(gated * gated, axis=2)
    unscaled = (gated * gate_gain[:, None, :]).astype(jnp.bfloat16)
    partial_out = jnp.einsum("mti,mid->mtd", unscaled, w_out, preferred_element_type=jnp.float32)
    extra = jnp.where(
        jnp.arange(128)[None, None, :] == 0, gate_squares[..., None], 0.0
    )
    summed = lax.psum_scatter(
        jnp.concatenate([partial_out, extra], axis=2), "mp", scatter_dimension=1, tiled=True
    )
    rows_here = summed.shape[1]
    gate_total = summed[:, :, D]
    mixed = summed[:, :, :D] * lax.rsqrt(gate_total[..., None] / INNER + EPS)
    mine = lax.dynamic_slice_in_dim(wide_in, mp_index * rows_here, rows_here, axis=1)
    final_part = rms_scale(mine + mixed, final_gain[:, None, :]).astype(jnp.bfloat16)
    seconds = [s[1](f) for s, f in zip(staged, firsts)]
    seconds, final_part = lax.optimization_barrier((seconds, final_part))
    final = lax.all_gather(final_part, "mp", axis=1, tiled=True)
    pieces = []
    for (_, _, sources), blocks in zip(staged, seconds):
        ordered = jnp.concatenate(
            [lax.dynamic_slice_in_dim(final, src * feat, feat, axis=2) for src in sources], axis=2
        )
        pieces.append(
            jnp.einsum("mtbd,bmvd->mtv", ordered.reshape(2, tokens, n_dp, feat), blocks,
                       preferred_element_type=jnp.float32)
        )
    logits = jnp.concatenate(pieces, axis=2)
    top_here = jnp.max(logits, axis=2)
    exp_here = jnp.sum(jnp.exp(logits - top_here[..., None]), axis=2)
    local_ids = targets - mp_index * vocab_local
    hit = jnp.arange(vocab_local, dtype=jnp.int32)[None, None, :] == local_ids[None, :, None]
    picked_here = jnp.sum(jnp.where(hit, logits, 0.0), axis=2)
    stats = lax.all_gather(jnp.stack([top_here, exp_here, picked_here]), "mp")
    top = jnp.max(stats[:, 0], axis=0)
    exp_total = jnp.sum(stats[:, 1] * jnp.exp(stats[:, 0] - top[None]), axis=0)
    picked = jnp.sum(stats[:, 2], axis=0)
    logprob = picked - (top + jnp.log(exp_total))
    token_ratio = logprob[0] - logprob[1]
    request_count = owners.shape[0]
    page_sums = lax.all_gather(jnp.sum(token_ratio.reshape(num_pages, PAGE), axis=1), "dp", tiled=True)
    request_ids = jnp.arange(request_count, dtype=jnp.int32)
    all_onehot = (page_request[:, None] == request_ids[None, :]).astype(jnp.float32)
    counts = jnp.sum(all_onehot, axis=0) * PAGE
    seq_mean = jnp.sum(page_sums[:, None] * all_onehot, axis=0) / counts
    owned = jnp.where(owners == dp_index, seq_mean, jnp.float32(0.0))[None, :]
    return (token_ratio, owned)


def solution(mesh):
    placed = (
        P(None, "dp", "mp"),
        P(),
        P(None, None, None, "mp"),
        P(),
        P(None, None, "mp"),
        P(None, None, "mp"),
        P(),
        P(None, "mp"),
        P(None, "mp"),
        P(None, "mp"),
        P(None, "mp"),
        P(None, "mp", None),
        P(),
        P(None, "mp", "dp"),
        P(),
        P("dp"),
        P(),
    )
    return jax.shard_map(
        local, mesh=mesh, in_specs=placed, out_specs=(P("dp"), P("dp", None)), check_vma=False
    )
```

```python
import jax
import jax.numpy as jnp
from jax import lax
from jax.sharding import PartitionSpec as P

D = 2048
INNER = 4096
HEADDIM = 64
STATE = 128
PAGE = 256


EPS = 1e-05
HIGH = lax.Precision.HIGHEST


def shifted(block, axis, distance):
    devices = range(lax.axis_size(axis))
    route = [(i - distance, i) for i in devices if i - distance in devices]
    return lax.ppermute(block, axis, route)


def entering(shard, axis, combine, identity):
    peers, index = (lax.axis_size(axis), lax.axis_index(axis))
    everything = jax.tree.map(lambda part: lax.all_gather(part, axis), shard)
    start = jax.tree.map(
        lambda part, zero: jnp.broadcast_to(jnp.asarray(zero, part.dtype), part.shape),
        shard,
        identity,
    )

    def turn(k, before):
        reached = k < index
        new = combine(before, jax.tree.map(lambda part: part[k], everything))
        return jax.tree.map(lambda a, b: jnp.where(reached, a, b), new, before)

    return lax.fori_loop(0, peers, turn, start)


def torus_gather(shard, axis, rows, cols, row_first):
    index = lax.axis_index(axis)
    row, col = (index // cols, index % cols)

    def step(block, along_rows, shifts):
        moved = [block]
        for s in shifts:
            if along_rows:
                route = [(r * cols + c, ((r + s) % rows) * cols + c) for r in range(rows) for c in range(cols)]
            else:
                route = [(r * cols + c, r * cols + (c + s) % cols) for r in range(rows) for c in range(cols)]
            moved.append(lax.ppermute(block, axis, route))
        return jnp.stack(moved)

    if row_first:
        sources = [((row - a) % rows) * cols + (col - b) % cols for b in range(cols) for a in range(rows)]
    else:
        sources = [((row - a) % rows) * cols + (col - b) % cols for a in range(rows) for b in range(cols)]

    def second(first):
        both = step(first, not row_first, range(1, cols if row_first else rows))
        return both.reshape((rows * cols,) + shard.shape)

    return step(shard, row_first, range(1, rows if row_first else cols)), second, sources


def rms_scale(rows, gain):
    mean_square = jnp.mean(rows * rows, axis=-1, keepdims=True)
    return rows * lax.rsqrt(mean_square + EPS) * gain


def page_conv(current, previous, weights):
    width = weights.shape[1]
    length = current.shape[2]
    padded = jnp.concatenate([previous, current], axis=2).astype(jnp.float32)
    total = padded[:, :, width - 1 : width - 1 + length, :] * weights[:, None, None, width - 1, :]
    for back in range(1, width):
        begin = width - 1 - back
        total = (
            total
            + padded[:, :, begin : begin + length, :] * weights[:, None, None, width - 1 - back, :]
        )
    return jax.nn.silu(total).astype(jnp.bfloat16)


def link_states(earlier, later):
    later_flag = later[0]
    keep = 1.0 - later_flag
    return (
        jnp.maximum(earlier[0], later_flag),
        later[1] * (later_flag + keep * earlier[1]),
        later[2] + keep * later[1][..., None, None] * earlier[2],
    )


def model_part(
    hidden_in,
    in_gain,
    w_zx,
    w_bc,
    w_dt,
    conv_x,
    conv_bc,
    dt_bias,
    a_rate,
    d_skip,
    gate_gain,
    w_out,
    final_gain,
    lm_head,
    page_request,
    targets,
    owners,
):
    n_dp = lax.axis_size("dp")
    dp_index = lax.axis_index("dp")
    mp_index = lax.axis_index("mp")
    tokens = hidden_in.shape[1]
    models = hidden_in.shape[0]
    num_pages = tokens // PAGE
    local_inner = w_zx.shape[3]
    local_heads = w_dt.shape[2]
    width = conv_x.shape[1]
    all_starts = page_request != jnp.concatenate([jnp.full((1,), -1, jnp.int32), page_request[:-1]])
    my_starts = lax.dynamic_slice_in_dim(all_starts, dp_index * num_pages, num_pages)
    my_req = lax.dynamic_slice_in_dim(page_request, dp_index * num_pages, num_pages)
    page_flags = my_starts.astype(jnp.float32)
    full_in = lax.all_gather(hidden_in, "mp", axis=2, tiled=True)
    wide_in = full_in.astype(jnp.float32)
    normed = rms_scale(wide_in, in_gain[:, None, :]).astype(jnp.bfloat16)
    zx_cols = w_zx.reshape(models, D, 2 * local_inner)
    proj_zx = jnp.einsum(
        "mtd,mde->mte", normed, zx_cols, preferred_element_type=jnp.float32
    ).astype(jnp.bfloat16)
    gate = proj_zx[:, :, :local_inner]
    values = proj_zx[:, :, local_inner:]
    proj_bc = jnp.einsum("mtd,mde->mte", normed, w_bc, preferred_element_type=jnp.float32).astype(
        jnp.bfloat16
    )
    proj_dt = jnp.einsum("mtd,mde->mte", normed, w_dt, preferred_element_type=jnp.float32).astype(
        jnp.bfloat16
    )
    rim_x, rim_bc = shifted(
        (values[:, tokens - (width - 1) :, :], proj_bc[:, tokens - (width - 1) :, :]), "dp", 1
    )
    value_pages = values.reshape(models, num_pages, PAGE, local_inner)
    bc_pages = proj_bc.reshape(models, num_pages, PAGE, 2 * STATE)
    cut_mask = my_starts[None, :, None, None]
    prev_x = jnp.concatenate([rim_x[:, None], value_pages[:, :-1, PAGE - (width - 1) :, :]], axis=1)
    prev_x = jnp.where(cut_mask, jnp.zeros_like(prev_x), prev_x)
    prev_bc = jnp.concatenate([rim_bc[:, None], bc_pages[:, :-1, PAGE - (width - 1) :, :]], axis=1)
    prev_bc = jnp.where(cut_mask, jnp.zeros_like(prev_bc), prev_bc)
    conv_values = page_conv(value_pages, prev_x, conv_x)
    conv_b_c = page_conv(bc_pages, prev_bc, conv_bc)
    step_size = jax.nn.softplus(proj_dt.astype(jnp.float32) + dt_bias[:, None, :])
    log_decay = -step_size * a_rate[:, None, :]
    x_pages = conv_values.astype(jnp.float32).reshape(models, num_pages, PAGE, local_heads, HEADDIM)
    b_pages = conv_b_c[..., :STATE].astype(jnp.float32)
    c_pages = conv_b_c[..., STATE:].astype(jnp.float32)
    dt_pages = step_size.reshape(models, num_pages, PAGE, local_heads)
    cum = jnp.cumsum(log_decay.reshape(models, num_pages, PAGE, local_heads), axis=2)
    inner = jnp.einsum("mkln,mksn->mkls", c_pages, b_pages, precision=HIGH)
    rows = jnp.arange(PAGE)
    lower = (rows[:, None] >= rows[None, :])[None, None, :, :, None]
    spread = cum[:, :, :, None, :] - cum[:, :, None, :, :]
    decay = jnp.where(lower, jnp.exp(jnp.where(lower, spread, 0.0)), 0.0)
    mixing = inner[..., None] * decay * dt_pages[:, :, None, :, :]
    y_intra = jnp.einsum("mklsh,mkshp->mklhp", mixing, x_pages, precision=HIGH)
    tail = jnp.exp(cum[:, :, -1:, :] - cum) * dt_pages
    page_end = jnp.einsum("mksh,mkshp,mksn->mkhpn", tail, x_pages, b_pages, precision=HIGH)
    page_decay = jnp.exp(cum[:, :, -1, :])
    summary = (
        jnp.zeros((1,), jnp.float32),
        jnp.ones((models, local_heads), jnp.float32),
        jnp.zeros((models, local_heads, HEADDIM, STATE), jnp.float32),
    )
    for page in range(num_pages):
        summary = link_states(
            summary, (page_flags[page : page + 1], page_decay[:, page], page_end[:, page])
        )
    gate_through = summary[1] * (1.0 - summary[0])
    lane = jnp.arange(STATE)[None, None, None, :] == 0
    packed = jnp.concatenate(
        [summary[2], jnp.where(lane, gate_through[..., None, None], 0.0)], axis=2
    )
    vocab_local = lm_head.shape[1]
    half = vocab_local // 2
    feat = lm_head.shape[2]
    staged = [
        torus_gather(part, "dp", 4, n_dp // 4, row_first)
        for row_first, part in ((False, lm_head[:, :half]), (True, lm_head[:, half:]))
    ]
    firsts, packed = lax.optimization_barrier(([s[0] for s in staged], packed))
    every = lax.all_gather(packed, "dp")
    ends = every[:, :, :, :HEADDIM, :]
    through = every[:, :, :, HEADDIM, 0]
    peers = jnp.arange(n_dp)
    factor = jnp.where((peers < dp_index)[:, None, None], through, 1.0)
    weight = jnp.flip(jnp.cumprod(jnp.flip(factor, 0), axis=0), 0)
    weight = jnp.concatenate([weight[1:], jnp.ones_like(weight[:1])], axis=0)
    weight = jnp.where((peers < dp_index)[:, None, None], weight, 0.0)
    carried = jnp.sum(weight[..., None, None] * ends, axis=0)
    state_in = (1.0 - page_flags[0]) * carried
    outputs = []
    for page in range(num_pages):
        if page > 0:
            state_in = (1.0 - page_flags[page]) * (
                page_decay[:, page - 1][..., None, None] * state_in + page_end[:, page - 1]
            )
        y_carry = jnp.exp(cum[:, page])[..., None] * jnp.einsum(
            "mln,mhpn->mlhp", c_pages[:, page], state_in, precision=HIGH
        )
        outputs.append(y_intra[:, page] + y_carry + d_skip[:, None, :, None] * x_pages[:, page])
    scanned = jnp.stack(outputs, axis=1).reshape(models, tokens, local_inner)
    gated = scanned * jax.nn.silu(gate.astype(jnp.float32))
    gate_squares = jnp.sum(gated * gated, axis=2)
    unscaled = (gated * gate_gain[:, None, :]).astype(jnp.bfloat16)
    partial_out = jnp.einsum("mti,mid->mtd", unscaled, w_out, preferred_element_type=jnp.float32)
    extra = jnp.where(
        jnp.arange(128)[None, None, :] == 0, gate_squares[..., None], 0.0
    )
    summed = lax.psum_scatter(
        jnp.concatenate([partial_out, extra], axis=2), "mp", scatter_dimension=1, tiled=True
    )
    rows_here = summed.shape[1]
    gate_total = summed[:, :, D]
    mixed = summed[:, :, :D] * lax.rsqrt(gate_total[..., None] / INNER + EPS)
    mine = lax.dynamic_slice_in_dim(wide_in, mp_index * rows_here, rows_here, axis=1)
    final_part = rms_scale(mine + mixed, final_gain[:, None, :]).astype(jnp.bfloat16)
    seconds = [s[1](f) for s, f in zip(staged, firsts)]
    seconds, final_part = lax.optimization_barrier((seconds, final_part))
    final = lax.all_gather(final_part, "mp", axis=1, tiled=True)
    pieces = []
    for (_, _, sources), blocks in zip(staged, seconds):
        ordered = jnp.concatenate(
            [lax.dynamic_slice_in_dim(final, src * feat, feat, axis=2) for src in sources], axis=2
        )
        pieces.append(
            jnp.einsum("mtbd,bmvd->mtv", ordered.reshape(models, tokens, n_dp, feat), blocks,
                       preferred_element_type=jnp.float32)
        )
    logits = jnp.concatenate(pieces, axis=2)
    top_here = jnp.max(logits, axis=2)
    exp_here = jnp.sum(jnp.exp(logits - top_here[..., None]), axis=2)
    local_ids = targets - mp_index * vocab_local
    hit = jnp.arange(vocab_local, dtype=jnp.int32)[None, None, :] == local_ids[None, :, None]
    picked_here = jnp.sum(jnp.where(hit, logits, 0.0), axis=2)
    return jnp.stack([top_here, exp_here, picked_here])


def local(*args):
    hidden_in = args[0]
    page_request, targets, owners = args[-3:]
    n_dp = lax.axis_size("dp")
    dp_index = lax.axis_index("dp")
    tokens = hidden_in.shape[1]
    num_pages = tokens // PAGE
    parts = [
        model_part(*[a[m : m + 1] for a in args[:-3]], page_request, targets, owners)
        for m in range(hidden_in.shape[0])
    ]
    here = jnp.concatenate(parts, axis=1)
    stats = lax.all_gather(here, "mp")
    top = jnp.max(stats[:, 0], axis=0)
    exp_total = jnp.sum(stats[:, 1] * jnp.exp(stats[:, 0] - top[None]), axis=0)
    picked = jnp.sum(stats[:, 2], axis=0)
    logprob = picked - (top + jnp.log(exp_total))
    token_ratio = logprob[0] - logprob[1]
    request_count = owners.shape[0]
    page_sums = lax.all_gather(jnp.sum(token_ratio.reshape(num_pages, PAGE), axis=1), "dp", tiled=True)
    request_ids = jnp.arange(request_count, dtype=jnp.int32)
    all_onehot = (page_request[:, None] == request_ids[None, :]).astype(jnp.float32)
    counts = jnp.sum(all_onehot, axis=0) * PAGE
    seq_mean = jnp.sum(page_sums[:, None] * all_onehot, axis=0) / counts
    owned = jnp.where(owners == dp_index, seq_mean, jnp.float32(0.0))[None, :]
    return (token_ratio, owned)


def solution(mesh):
    placed = (
        P(None, "dp", "mp"),
        P(),
        P(None, None, None, "mp"),
        P(),
        P(None, None, "mp"),
        P(None, None, "mp"),
        P(),
        P(None, "mp"),
        P(None, "mp"),
        P(None, "mp"),
        P(None, "mp"),
        P(None, "mp", None),
        P(),
        P(None, "mp", "dp"),
        P(),
        P("dp"),
        P(),
    )
    return jax.shard_map(
        local, mesh=mesh, in_specs=placed, out_specs=(P("dp"), P("dp", None)), check_vma=False
    )
```

```python
import jax
import jax.numpy as jnp
from jax import lax
from jax.sharding import PartitionSpec as P

D = 2048
INNER = 4096
HEADDIM = 64
STATE = 128
PAGE = 256


EPS = 1e-05
HIGH = lax.Precision.HIGHEST


def shifted(block, axis, distance):
    devices = range(lax.axis_size(axis))
    route = [(i - distance, i) for i in devices if i - distance in devices]
    return lax.ppermute(block, axis, route)


def entering(shard, axis, combine, identity):
    peers, index = (lax.axis_size(axis), lax.axis_index(axis))
    everything = jax.tree.map(lambda part: lax.all_gather(part, axis), shard)
    start = jax.tree.map(
        lambda part, zero: jnp.broadcast_to(jnp.asarray(zero, part.dtype), part.shape),
        shard,
        identity,
    )

    def turn(k, before):
        reached = k < index
        new = combine(before, jax.tree.map(lambda part: part[k], everything))
        return jax.tree.map(lambda a, b: jnp.where(reached, a, b), new, before)

    return lax.fori_loop(0, peers, turn, start)


def torus_gather(shard, axis, rows, cols, row_first):
    index = lax.axis_index(axis)
    row, col = (index // cols, index % cols)

    def step(block, along_rows, shifts):
        moved = [block]
        for s in shifts:
            if along_rows:
                route = [(r * cols + c, ((r + s) % rows) * cols + c) for r in range(rows) for c in range(cols)]
            else:
                route = [(r * cols + c, r * cols + (c + s) % cols) for r in range(rows) for c in range(cols)]
            moved.append(lax.ppermute(block, axis, route))
        return jnp.stack(moved)

    if row_first:
        sources = [((row - a) % rows) * cols + (col - b) % cols for b in range(cols) for a in range(rows)]
    else:
        sources = [((row - a) % rows) * cols + (col - b) % cols for a in range(rows) for b in range(cols)]

    def second(first):
        both = step(first, not row_first, range(1, cols if row_first else rows))
        return both.reshape((rows * cols,) + shard.shape)

    return step(shard, row_first, range(1, rows if row_first else cols)), second, sources


def rms_scale(rows, gain):
    mean_square = jnp.mean(rows * rows, axis=-1, keepdims=True)
    return rows * lax.rsqrt(mean_square + EPS) * gain


def page_conv(current, previous, weights):
    width = weights.shape[1]
    length = current.shape[2]
    padded = jnp.concatenate([previous, current], axis=2).astype(jnp.float32)
    total = padded[:, :, width - 1 : width - 1 + length, :] * weights[:, None, None, width - 1, :]
    for back in range(1, width):
        begin = width - 1 - back
        total = (
            total
            + padded[:, :, begin : begin + length, :] * weights[:, None, None, width - 1 - back, :]
        )
    return jax.nn.silu(total).astype(jnp.bfloat16)


def link_states(earlier, later):
    later_flag = later[0]
    keep = 1.0 - later_flag
    return (
        jnp.maximum(earlier[0], later_flag),
        later[1] * (later_flag + keep * earlier[1]),
        later[2] + keep * later[1][..., None, None] * earlier[2],
    )


def local(
    hidden_in,
    in_gain,
    w_zx,
    w_bc,
    w_dt,
    conv_x,
    conv_bc,
    dt_bias,
    a_rate,
    d_skip,
    gate_gain,
    w_out,
    final_gain,
    lm_head,
    page_request,
    targets,
    owners,
):
    n_dp = lax.axis_size("dp")
    dp_index = lax.axis_index("dp")
    mp_index = lax.axis_index("mp")
    tokens = hidden_in.shape[1]
    num_pages = tokens // PAGE
    local_inner = w_zx.shape[3]
    local_heads = w_dt.shape[2]
    width = conv_x.shape[1]
    all_starts = page_request != jnp.concatenate([jnp.full((1,), -1, jnp.int32), page_request[:-1]])
    my_starts = lax.dynamic_slice_in_dim(all_starts, dp_index * num_pages, num_pages)
    my_req = lax.dynamic_slice_in_dim(page_request, dp_index * num_pages, num_pages)
    page_flags = my_starts.astype(jnp.float32)
    full_in = lax.all_gather(hidden_in, "mp", axis=2, tiled=True)
    vocab_local = lm_head.shape[1]
    half = vocab_local // 2
    feat = lm_head.shape[2]
    staged = [
        torus_gather(part, "dp", 4, n_dp // 4, row_first)
        for row_first, part in ((False, lm_head[:, :half]), (True, lm_head[:, half:]))
    ]
    firsts, full_in = lax.optimization_barrier(([s[0] for s in staged], full_in))
    wide_in = full_in.astype(jnp.float32)
    normed = rms_scale(wide_in, in_gain[:, None, :]).astype(jnp.bfloat16)
    zx_cols = w_zx.reshape(2, D, 2 * local_inner)
    proj_zx = jnp.einsum(
        "mtd,mde->mte", normed, zx_cols, preferred_element_type=jnp.float32
    ).astype(jnp.bfloat16)
    gate = proj_zx[:, :, :local_inner]
    values = proj_zx[:, :, local_inner:]
    proj_bc = jnp.einsum("mtd,mde->mte", normed, w_bc, preferred_element_type=jnp.float32).astype(
        jnp.bfloat16
    )
    proj_dt = jnp.einsum("mtd,mde->mte", normed, w_dt, preferred_element_type=jnp.float32).astype(
        jnp.bfloat16
    )
    rim_x, rim_bc = shifted(
        (values[:, tokens - (width - 1) :, :], proj_bc[:, tokens - (width - 1) :, :]), "dp", 1
    )
    value_pages = values.reshape(2, num_pages, PAGE, local_inner)
    bc_pages = proj_bc.reshape(2, num_pages, PAGE, 2 * STATE)
    cut_mask = my_starts[None, :, None, None]
    prev_x = jnp.concatenate([rim_x[:, None], value_pages[:, :-1, PAGE - (width - 1) :, :]], axis=1)
    prev_x = jnp.where(cut_mask, jnp.zeros_like(prev_x), prev_x)
    prev_bc = jnp.concatenate([rim_bc[:, None], bc_pages[:, :-1, PAGE - (width - 1) :, :]], axis=1)
    prev_bc = jnp.where(cut_mask, jnp.zeros_like(prev_bc), prev_bc)
    conv_values = page_conv(value_pages, prev_x, conv_x)
    conv_b_c = page_conv(bc_pages, prev_bc, conv_bc)
    step_size = jax.nn.softplus(proj_dt.astype(jnp.float32) + dt_bias[:, None, :])
    log_decay = -step_size * a_rate[:, None, :]
    x_pages = conv_values.astype(jnp.float32).reshape(2, num_pages, PAGE, local_heads, HEADDIM)
    b_pages = conv_b_c[..., :STATE].astype(jnp.float32)
    c_pages = conv_b_c[..., STATE:].astype(jnp.float32)
    dt_pages = step_size.reshape(2, num_pages, PAGE, local_heads)
    cum = jnp.cumsum(log_decay.reshape(2, num_pages, PAGE, local_heads), axis=2)
    inner = jnp.einsum("mkln,mksn->mkls", c_pages, b_pages, precision=HIGH)
    rows = jnp.arange(PAGE)
    lower = (rows[:, None] >= rows[None, :])[None, None, :, :, None]
    spread = cum[:, :, :, None, :] - cum[:, :, None, :, :]
    decay = jnp.where(lower, jnp.exp(jnp.where(lower, spread, 0.0)), 0.0)
    mixing = inner[..., None] * decay * dt_pages[:, :, None, :, :]
    y_intra = jnp.einsum("mklsh,mkshp->mklhp", mixing, x_pages, precision=HIGH)
    tail = jnp.exp(cum[:, :, -1:, :] - cum) * dt_pages
    page_end = jnp.einsum("mksh,mkshp,mksn->mkhpn", tail, x_pages, b_pages, precision=HIGH)
    page_decay = jnp.exp(cum[:, :, -1, :])
    summary = (
        jnp.zeros((1,), jnp.float32),
        jnp.ones((2, local_heads), jnp.float32),
        jnp.zeros((2, local_heads, HEADDIM, STATE), jnp.float32),
    )
    for page in range(num_pages):
        summary = link_states(
            summary, (page_flags[page : page + 1], page_decay[:, page], page_end[:, page])
        )
    gate_through = summary[1] * (1.0 - summary[0])
    lane = jnp.arange(STATE)[None, None, None, :] == 0
    packed = jnp.concatenate(
        [summary[2], jnp.where(lane, gate_through[..., None, None], 0.0)], axis=2
    )
    seconds = [s[1](f) for s, f in zip(staged, firsts)]
    seconds, packed = lax.optimization_barrier((seconds, packed))
    every = lax.all_gather(packed, "dp")
    ends = every[:, :, :, :HEADDIM, :]
    through = every[:, :, :, HEADDIM, 0]
    peers = jnp.arange(n_dp)
    factor = jnp.where((peers < dp_index)[:, None, None], through, 1.0)
    weight = jnp.flip(jnp.cumprod(jnp.flip(factor, 0), axis=0), 0)
    weight = jnp.concatenate([weight[1:], jnp.ones_like(weight[:1])], axis=0)
    weight = jnp.where((peers < dp_index)[:, None, None], weight, 0.0)
    carried = jnp.sum(weight[..., None, None] * ends, axis=0)
    state_in = (1.0 - page_flags[0]) * carried
    outputs = []
    for page in range(num_pages):
        if page > 0:
            state_in = (1.0 - page_flags[page]) * (
                page_decay[:, page - 1][..., None, None] * state_in + page_end[:, page - 1]
            )
        y_carry = jnp.exp(cum[:, page])[..., None] * jnp.einsum(
            "mln,mhpn->mlhp", c_pages[:, page], state_in, precision=HIGH
        )
        outputs.append(y_intra[:, page] + y_carry + d_skip[:, None, :, None] * x_pages[:, page])
    scanned = jnp.stack(outputs, axis=1).reshape(2, tokens, local_inner)
    gated = scanned * jax.nn.silu(gate.astype(jnp.float32))
    gate_squares = jnp.sum(gated * gated, axis=2)
    unscaled = (gated * gate_gain[:, None, :]).astype(jnp.bfloat16)
    partial_out = jnp.einsum("mti,mid->mtd", unscaled, w_out, preferred_element_type=jnp.float32)
    extra = jnp.where(
        jnp.arange(128)[None, None, :] == 0, gate_squares[..., None], 0.0
    )
    summed = lax.psum_scatter(
        jnp.concatenate([partial_out, extra], axis=2), "mp", scatter_dimension=1, tiled=True
    )
    rows_here = summed.shape[1]
    gate_total = summed[:, :, D]
    mixed = summed[:, :, :D] * lax.rsqrt(gate_total[..., None] / INNER + EPS)
    mine = lax.dynamic_slice_in_dim(wide_in, mp_index * rows_here, rows_here, axis=1)
    final_part = rms_scale(mine + mixed, final_gain[:, None, :]).astype(jnp.bfloat16)
    final = lax.all_gather(final_part, "mp", axis=1, tiled=True)
    pieces = []
    for (_, _, sources), blocks in zip(staged, seconds):
        ordered = jnp.concatenate(
            [lax.dynamic_slice_in_dim(final, src * feat, feat, axis=2) for src in sources], axis=2
        )
        pieces.append(
            jnp.einsum("mtbd,bmvd->mtv", ordered.reshape(2, tokens, n_dp, feat), blocks,
                       preferred_element_type=jnp.float32)
        )
    logits = jnp.concatenate(pieces, axis=2)
    top_here = jnp.max(logits, axis=2)
    exp_here = jnp.sum(jnp.exp(logits - top_here[..., None]), axis=2)
    local_ids = targets - mp_index * vocab_local
    hit = jnp.arange(vocab_local, dtype=jnp.int32)[None, None, :] == local_ids[None, :, None]
    picked_here = jnp.sum(jnp.where(hit, logits, 0.0), axis=2)
    stats = lax.all_gather(jnp.stack([top_here, exp_here, picked_here]), "mp")
    top = jnp.max(stats[:, 0], axis=0)
    exp_total = jnp.sum(stats[:, 1] * jnp.exp(stats[:, 0] - top[None]), axis=0)
    picked = jnp.sum(stats[:, 2], axis=0)
    logprob = picked - (top + jnp.log(exp_total))
    token_ratio = logprob[0] - logprob[1]
    request_count = owners.shape[0]
    page_sums = lax.all_gather(jnp.sum(token_ratio.reshape(num_pages, PAGE), axis=1), "dp", tiled=True)
    request_ids = jnp.arange(request_count, dtype=jnp.int32)
    all_onehot = (page_request[:, None] == request_ids[None, :]).astype(jnp.float32)
    counts = jnp.sum(all_onehot, axis=0) * PAGE
    seq_mean = jnp.sum(page_sums[:, None] * all_onehot, axis=0) / counts
    owned = jnp.where(owners == dp_index, seq_mean, jnp.float32(0.0))[None, :]
    return (token_ratio, owned)


def solution(mesh):
    placed = (
        P(None, "dp", "mp"),
        P(),
        P(None, None, None, "mp"),
        P(),
        P(None, None, "mp"),
        P(None, None, "mp"),
        P(),
        P(None, "mp"),
        P(None, "mp"),
        P(None, "mp"),
        P(None, "mp"),
        P(None, "mp", None),
        P(),
        P(None, "mp", "dp"),
        P(),
        P("dp"),
        P(),
    )
    return jax.shard_map(
        local, mesh=mesh, in_specs=placed, out_specs=(P("dp"), P("dp", None)), check_vma=False
    )
```

```python
import jax
import jax.numpy as jnp
from jax import lax
from jax.sharding import PartitionSpec as P

D = 2048
INNER = 4096
HEADDIM = 64
STATE = 128
PAGE = 256


EPS = 1e-05
HIGH = lax.Precision.HIGHEST


def shifted(block, axis, distance):
    devices = range(lax.axis_size(axis))
    route = [(i - distance, i) for i in devices if i - distance in devices]
    return lax.ppermute(block, axis, route)


def entering(shard, axis, combine, identity):
    peers, index = (lax.axis_size(axis), lax.axis_index(axis))
    everything = jax.tree.map(lambda part: lax.all_gather(part, axis), shard)
    start = jax.tree.map(
        lambda part, zero: jnp.broadcast_to(jnp.asarray(zero, part.dtype), part.shape),
        shard,
        identity,
    )

    def turn(k, before):
        reached = k < index
        new = combine(before, jax.tree.map(lambda part: part[k], everything))
        return jax.tree.map(lambda a, b: jnp.where(reached, a, b), new, before)

    return lax.fori_loop(0, peers, turn, start)


def torus_gather(shard, axis, rows, cols, row_first):
    index = lax.axis_index(axis)
    row, col = (index // cols, index % cols)

    def step(block, along_rows, shifts):
        moved = [block]
        for s in shifts:
            if along_rows:
                route = [(r * cols + c, ((r + s) % rows) * cols + c) for r in range(rows) for c in range(cols)]
            else:
                route = [(r * cols + c, r * cols + (c + s) % cols) for r in range(rows) for c in range(cols)]
            moved.append(lax.ppermute(block, axis, route))
        return jnp.stack(moved)

    if row_first:
        sources = [((row - a) % rows) * cols + (col - b) % cols for b in range(cols) for a in range(rows)]
    else:
        sources = [((row - a) % rows) * cols + (col - b) % cols for a in range(rows) for b in range(cols)]

    def second(first):
        both = step(first, not row_first, range(1, cols if row_first else rows))
        return both.reshape((rows * cols,) + shard.shape)

    return step(shard, row_first, range(1, rows if row_first else cols)), second, sources


def rms_scale(rows, gain):
    mean_square = jnp.mean(rows * rows, axis=-1, keepdims=True)
    return rows * lax.rsqrt(mean_square + EPS) * gain


def page_conv(current, previous, weights):
    width = weights.shape[1]
    length = current.shape[2]
    padded = jnp.concatenate([previous, current], axis=2).astype(jnp.float32)
    total = padded[:, :, width - 1 : width - 1 + length, :] * weights[:, None, None, width - 1, :]
    for back in range(1, width):
        begin = width - 1 - back
        total = (
            total
            + padded[:, :, begin : begin + length, :] * weights[:, None, None, width - 1 - back, :]
        )
    return jax.nn.silu(total).astype(jnp.bfloat16)


def link_states(earlier, later):
    later_flag = later[0]
    keep = 1.0 - later_flag
    return (
        jnp.maximum(earlier[0], later_flag),
        later[1] * (later_flag + keep * earlier[1]),
        later[2] + keep * later[1][..., None, None] * earlier[2],
    )


def local(
    hidden_in,
    in_gain,
    w_zx,
    w_bc,
    w_dt,
    conv_x,
    conv_bc,
    dt_bias,
    a_rate,
    d_skip,
    gate_gain,
    w_out,
    final_gain,
    lm_head,
    page_request,
    targets,
    owners,
):
    n_dp = lax.axis_size("dp")
    dp_index = lax.axis_index("dp")
    mp_index = lax.axis_index("mp")
    tokens = hidden_in.shape[1]
    num_pages = tokens // PAGE
    local_inner = w_zx.shape[3]
    local_heads = w_dt.shape[2]
    width = conv_x.shape[1]
    all_starts = page_request != jnp.concatenate([jnp.full((1,), -1, jnp.int32), page_request[:-1]])
    my_starts = lax.dynamic_slice_in_dim(all_starts, dp_index * num_pages, num_pages)
    my_req = lax.dynamic_slice_in_dim(page_request, dp_index * num_pages, num_pages)
    page_flags = my_starts.astype(jnp.float32)
    full_in = lax.all_gather(hidden_in, "mp", axis=2, tiled=True)
    wide_in = full_in.astype(jnp.float32)
    normed = rms_scale(wide_in, in_gain[:, None, :]).astype(jnp.bfloat16)
    zx_cols = w_zx.reshape(2, D, 2 * local_inner)
    proj_zx = jnp.einsum(
        "mtd,mde->mte", normed, zx_cols, preferred_element_type=jnp.float32
    ).astype(jnp.bfloat16)
    gate = proj_zx[:, :, :local_inner]
    values = proj_zx[:, :, local_inner:]
    proj_bc = jnp.einsum("mtd,mde->mte", normed, w_bc, preferred_element_type=jnp.float32).astype(
        jnp.bfloat16
    )
    proj_dt = jnp.einsum("mtd,mde->mte", normed, w_dt, preferred_element_type=jnp.float32).astype(
        jnp.bfloat16
    )
    rim_x, rim_bc = shifted(
        (values[:, tokens - (width - 1) :, :], proj_bc[:, tokens - (width - 1) :, :]), "dp", 1
    )
    value_pages = values.reshape(2, num_pages, PAGE, local_inner)
    bc_pages = proj_bc.reshape(2, num_pages, PAGE, 2 * STATE)
    cut_mask = my_starts[None, :, None, None]
    prev_x = jnp.concatenate([rim_x[:, None], value_pages[:, :-1, PAGE - (width - 1) :, :]], axis=1)
    prev_x = jnp.where(cut_mask, jnp.zeros_like(prev_x), prev_x)
    prev_bc = jnp.concatenate([rim_bc[:, None], bc_pages[:, :-1, PAGE - (width - 1) :, :]], axis=1)
    prev_bc = jnp.where(cut_mask, jnp.zeros_like(prev_bc), prev_bc)
    conv_values = page_conv(value_pages, prev_x, conv_x)
    conv_b_c = page_conv(bc_pages, prev_bc, conv_bc)
    step_size = jax.nn.softplus(proj_dt.astype(jnp.float32) + dt_bias[:, None, :])
    log_decay = -step_size * a_rate[:, None, :]
    x_pages = conv_values.astype(jnp.float32).reshape(2, num_pages, PAGE, local_heads, HEADDIM)
    b_pages = conv_b_c[..., :STATE].astype(jnp.float32)
    c_pages = conv_b_c[..., STATE:].astype(jnp.float32)
    dt_pages = step_size.reshape(2, num_pages, PAGE, local_heads)
    cum = jnp.cumsum(log_decay.reshape(2, num_pages, PAGE, local_heads), axis=2)
    inner = jnp.einsum("mkln,mksn->mkls", c_pages, b_pages, precision=HIGH)
    rows = jnp.arange(PAGE)
    lower = (rows[:, None] >= rows[None, :])[None, None, :, :, None]
    spread = cum[:, :, :, None, :] - cum[:, :, None, :, :]
    decay = jnp.where(lower, jnp.exp(jnp.where(lower, spread, 0.0)), 0.0)
    mixing = inner[..., None] * decay * dt_pages[:, :, None, :, :]
    y_intra = jnp.einsum("mklsh,mkshp->mklhp", mixing, x_pages, precision=HIGH)
    tail = jnp.exp(cum[:, :, -1:, :] - cum) * dt_pages
    page_end = jnp.einsum("mksh,mkshp,mksn->mkhpn", tail, x_pages, b_pages, precision=HIGH)
    page_decay = jnp.exp(cum[:, :, -1, :])
    summary = (
        jnp.zeros((1,), jnp.float32),
        jnp.ones((2, local_heads), jnp.float32),
        jnp.zeros((2, local_heads, HEADDIM, STATE), jnp.float32),
    )
    for page in range(num_pages):
        summary = link_states(
            summary, (page_flags[page : page + 1], page_decay[:, page], page_end[:, page])
        )
    gate_through = summary[1] * (1.0 - summary[0])
    lane = jnp.arange(STATE)[None, None, None, :] == 0
    packed = jnp.concatenate(
        [summary[2], jnp.where(lane, gate_through[..., None, None], 0.0)], axis=2
    )
    vocab_local = lm_head.shape[1]
    half = vocab_local // 2
    feat = lm_head.shape[2]
    staged = [
        torus_gather(part, "dp", 4, n_dp // 4, row_first)
        for row_first, part in ((False, lm_head[:, :half]), (True, lm_head[:, half:]))
    ]
    firsts, packed = lax.optimization_barrier(([s[0] for s in staged], packed))
    every = lax.all_gather(packed, "dp")
    ends = every[:, :, :, :HEADDIM, :]
    through = every[:, :, :, HEADDIM, 0]
    peers = jnp.arange(n_dp)
    factor = jnp.where((peers < dp_index)[:, None, None], through, 1.0)
    weight = jnp.flip(jnp.cumprod(jnp.flip(factor, 0), axis=0), 0)
    weight = jnp.concatenate([weight[1:], jnp.ones_like(weight[:1])], axis=0)
    weight = jnp.where((peers < dp_index)[:, None, None], weight, 0.0)
    carried = jnp.sum(weight[..., None, None] * ends, axis=0)
    state_in = (1.0 - page_flags[0]) * carried
    outputs = []
    for page in range(num_pages):
        if page > 0:
            state_in = (1.0 - page_flags[page]) * (
                page_decay[:, page - 1][..., None, None] * state_in + page_end[:, page - 1]
            )
        y_carry = jnp.exp(cum[:, page])[..., None] * jnp.einsum(
            "mln,mhpn->mlhp", c_pages[:, page], state_in, precision=HIGH
        )
        outputs.append(y_intra[:, page] + y_carry + d_skip[:, None, :, None] * x_pages[:, page])
    scanned = jnp.stack(outputs, axis=1).reshape(2, tokens, local_inner)
    gated = scanned * jax.nn.silu(gate.astype(jnp.float32))
    gate_squares = jnp.sum(gated * gated, axis=2)
    unscaled = (gated * gate_gain[:, None, :]).astype(jnp.bfloat16)
    partial_out = jnp.einsum("mti,mid->mtd", unscaled, w_out, preferred_element_type=jnp.float32)
    extra = jnp.where(
        jnp.arange(128)[None, None, :] == 0, gate_squares[..., None], 0.0
    )
    summed = lax.psum_scatter(
        jnp.concatenate([partial_out, extra], axis=2), "mp", scatter_dimension=1, tiled=True
    )
    rows_here = summed.shape[1]
    gate_total = summed[:, :, D]
    mixed = summed[:, :, :D] * lax.rsqrt(gate_total[..., None] / INNER + EPS)
    mine = lax.dynamic_slice_in_dim(wide_in, mp_index * rows_here, rows_here, axis=1)
    final_part = rms_scale(mine + mixed, final_gain[:, None, :]).astype(jnp.bfloat16)
    seconds = [s[1](f) for s, f in zip(staged, firsts)]
    seconds, final_part = lax.optimization_barrier((seconds, final_part))
    grid_rows, grid_cols = (4, n_dp // 4)
    final_part = jnp.take(
        final_part.reshape(2, rows_here, n_dp, feat), jnp.stack(staged[0][2]), axis=2
    ).reshape(final_part.shape)
    final = lax.all_gather(final_part, "mp", axis=1, tiled=True)
    by_rows = final.reshape(2, tokens, grid_rows, grid_cols, feat)
    logits = jnp.concatenate(
        [
            jnp.einsum("mtabd,abmvd->mtv", by_rows,
                       seconds[0].reshape((grid_rows, grid_cols) + seconds[0].shape[1:]),
                       preferred_element_type=jnp.float32),
            jnp.einsum("mtabd,bamvd->mtv", by_rows,
                       seconds[1].reshape((grid_cols, grid_rows) + seconds[1].shape[1:]),
                       preferred_element_type=jnp.float32),
        ],
        axis=2,
    )
    top_here = jnp.max(logits, axis=2)
    exp_here = jnp.sum(jnp.exp(logits - top_here[..., None]), axis=2)
    local_ids = targets - mp_index * vocab_local
    hit = jnp.arange(vocab_local, dtype=jnp.int32)[None, None, :] == local_ids[None, :, None]
    picked_here = jnp.sum(jnp.where(hit, logits, 0.0), axis=2)
    stats = lax.all_gather(jnp.stack([top_here, exp_here, picked_here]), "mp")
    top = jnp.max(stats[:, 0], axis=0)
    exp_total = jnp.sum(stats[:, 1] * jnp.exp(stats[:, 0] - top[None]), axis=0)
    picked = jnp.sum(stats[:, 2], axis=0)
    logprob = picked - (top + jnp.log(exp_total))
    token_ratio = logprob[0] - logprob[1]
    request_count = owners.shape[0]
    page_sums = jnp.sum(token_ratio.reshape(num_pages, PAGE), axis=1)
    request_ids = jnp.arange(request_count, dtype=jnp.int32)
    all_onehot = (page_request[:, None] == request_ids[None, :]).astype(jnp.float32)
    counts = jnp.sum(all_onehot, axis=0) * PAGE
    my_onehot = (my_req[:, None] == request_ids[None, :]).astype(jnp.float32)
    seq_mean = jnp.sum(page_sums[:, None] * my_onehot, axis=0) / counts
    if n_dp & (n_dp - 1) == 0:
        bit = 1
        while bit < n_dp:
            seq_mean = seq_mean + lax.ppermute(seq_mean, "dp", [(i, i ^ bit) for i in range(n_dp)])
            bit *= 2
    else:
        seq_mean = lax.psum(seq_mean, "dp")
    owned = jnp.where(owners == dp_index, seq_mean, jnp.float32(0.0))[None, :]
    return (token_ratio, owned)


def solution(mesh):
    placed = (
        P(None, "dp", "mp"),
        P(),
        P(None, None, None, "mp"),
        P(),
        P(None, None, "mp"),
        P(None, None, "mp"),
        P(),
        P(None, "mp"),
        P(None, "mp"),
        P(None, "mp"),
        P(None, "mp"),
        P(None, "mp", None),
        P(),
        P(None, "mp", "dp"),
        P(),
        P("dp"),
        P(),
    )
    return jax.shard_map(
        local, mesh=mesh, in_specs=placed, out_specs=(P("dp"), P("dp", None)), check_vma=False
    )
```

```python
import jax
import jax.numpy as jnp
from jax import lax
from jax.sharding import PartitionSpec as P

D = 2048
INNER = 4096
HEADDIM = 64
STATE = 128
PAGE = 256


EPS = 1e-05
HIGH = lax.Precision.HIGHEST


def shifted(block, axis, distance):
    devices = range(lax.axis_size(axis))
    route = [(i - distance, i) for i in devices if i - distance in devices]
    return lax.ppermute(block, axis, route)


def entering(shard, axis, combine, identity):
    peers, index = (lax.axis_size(axis), lax.axis_index(axis))
    everything = jax.tree.map(lambda part: lax.all_gather(part, axis), shard)
    start = jax.tree.map(
        lambda part, zero: jnp.broadcast_to(jnp.asarray(zero, part.dtype), part.shape),
        shard,
        identity,
    )

    def turn(k, before):
        reached = k < index
        new = combine(before, jax.tree.map(lambda part: part[k], everything))
        return jax.tree.map(lambda a, b: jnp.where(reached, a, b), new, before)

    return lax.fori_loop(0, peers, turn, start)


def torus_gather(shard, axis, rows, cols, row_first):
    index = lax.axis_index(axis)
    row, col = (index // cols, index % cols)

    def step(block, along_rows, shifts, stacked=True):
        moved = [block]
        for s in shifts:
            if along_rows:
                route = [(r * cols + c, ((r + s) % rows) * cols + c) for r in range(rows) for c in range(cols)]
            else:
                route = [(r * cols + c, r * cols + (c + s) % cols) for r in range(rows) for c in range(cols)]
            moved.append(lax.ppermute(block, axis, route))
        return jnp.stack(moved) if stacked else moved

    if row_first:
        sources = [((row - a) % rows) * cols + (col - b) % cols for b in range(cols) for a in range(rows)]
    else:
        sources = [((row - a) % rows) * cols + (col - b) % cols for a in range(rows) for b in range(cols)]

    def second(first):
        return step(first, not row_first, range(1, cols if row_first else rows), stacked=False)

    return step(shard, row_first, range(1, rows if row_first else cols)), second, sources


def rms_scale(rows, gain):
    mean_square = jnp.mean(rows * rows, axis=-1, keepdims=True)
    return rows * lax.rsqrt(mean_square + EPS) * gain


def page_conv(current, previous, weights):
    width = weights.shape[1]
    length = current.shape[2]
    padded = jnp.concatenate([previous, current], axis=2).astype(jnp.float32)
    total = padded[:, :, width - 1 : width - 1 + length, :] * weights[:, None, None, width - 1, :]
    for back in range(1, width):
        begin = width - 1 - back
        total = (
            total
            + padded[:, :, begin : begin + length, :] * weights[:, None, None, width - 1 - back, :]
        )
    return jax.nn.silu(total).astype(jnp.bfloat16)


def link_states(earlier, later):
    later_flag = later[0]
    keep = 1.0 - later_flag
    return (
        jnp.maximum(earlier[0], later_flag),
        later[1] * (later_flag + keep * earlier[1]),
        later[2] + keep * later[1][..., None, None] * earlier[2],
    )


def local(
    hidden_in,
    in_gain,
    w_zx,
    w_bc,
    w_dt,
    conv_x,
    conv_bc,
    dt_bias,
    a_rate,
    d_skip,
    gate_gain,
    w_out,
    final_gain,
    lm_head,
    page_request,
    targets,
    owners,
):
    n_dp = lax.axis_size("dp")
    dp_index = lax.axis_index("dp")
    mp_index = lax.axis_index("mp")
    tokens = hidden_in.shape[1]
    num_pages = tokens // PAGE
    local_inner = w_zx.shape[3]
    local_heads = w_dt.shape[2]
    width = conv_x.shape[1]
    all_starts = page_request != jnp.concatenate([jnp.full((1,), -1, jnp.int32), page_request[:-1]])
    my_starts = lax.dynamic_slice_in_dim(all_starts, dp_index * num_pages, num_pages)
    my_req = lax.dynamic_slice_in_dim(page_request, dp_index * num_pages, num_pages)
    page_flags = my_starts.astype(jnp.float32)
    full_in = lax.all_gather(hidden_in, "mp", axis=2, tiled=True)
    wide_in = full_in.astype(jnp.float32)
    normed = rms_scale(wide_in, in_gain[:, None, :]).astype(jnp.bfloat16)
    zx_cols = w_zx.reshape(2, D, 2 * local_inner)
    proj_zx = jnp.einsum(
        "mtd,mde->mte", normed, zx_cols, preferred_element_type=jnp.float32
    ).astype(jnp.bfloat16)
    gate = proj_zx[:, :, :local_inner]
    values = proj_zx[:, :, local_inner:]
    proj_bc = jnp.einsum("mtd,mde->mte", normed, w_bc, preferred_element_type=jnp.float32).astype(
        jnp.bfloat16
    )
    proj_dt = jnp.einsum("mtd,mde->mte", normed, w_dt, preferred_element_type=jnp.float32).astype(
        jnp.bfloat16
    )
    rim_x, rim_bc = shifted(
        (values[:, tokens - (width - 1) :, :], proj_bc[:, tokens - (width - 1) :, :]), "dp", 1
    )
    value_pages = values.reshape(2, num_pages, PAGE, local_inner)
    bc_pages = proj_bc.reshape(2, num_pages, PAGE, 2 * STATE)
    cut_mask = my_starts[None, :, None, None]
    prev_x = jnp.concatenate([rim_x[:, None], value_pages[:, :-1, PAGE - (width - 1) :, :]], axis=1)
    prev_x = jnp.where(cut_mask, jnp.zeros_like(prev_x), prev_x)
    prev_bc = jnp.concatenate([rim_bc[:, None], bc_pages[:, :-1, PAGE - (width - 1) :, :]], axis=1)
    prev_bc = jnp.where(cut_mask, jnp.zeros_like(prev_bc), prev_bc)
    conv_values = page_conv(value_pages, prev_x, conv_x)
    conv_b_c = page_conv(bc_pages, prev_bc, conv_bc)
    step_size = jax.nn.softplus(proj_dt.astype(jnp.float32) + dt_bias[:, None, :])
    log_decay = -step_size * a_rate[:, None, :]
    x_pages = conv_values.astype(jnp.float32).reshape(2, num_pages, PAGE, local_heads, HEADDIM)
    b_pages = conv_b_c[..., :STATE].astype(jnp.float32)
    c_pages = conv_b_c[..., STATE:].astype(jnp.float32)
    dt_pages = step_size.reshape(2, num_pages, PAGE, local_heads)
    cum = jnp.cumsum(log_decay.reshape(2, num_pages, PAGE, local_heads), axis=2)
    inner = jnp.einsum("mkln,mksn->mkls", c_pages, b_pages, precision=HIGH)
    rows = jnp.arange(PAGE)
    lower = (rows[:, None] >= rows[None, :])[None, None, :, :, None]
    spread = cum[:, :, :, None, :] - cum[:, :, None, :, :]
    decay = jnp.where(lower, jnp.exp(jnp.where(lower, spread, 0.0)), 0.0)
    mixing = inner[..., None] * decay * dt_pages[:, :, None, :, :]
    y_intra = jnp.einsum("mklsh,mkshp->mklhp", mixing, x_pages, precision=HIGH)
    tail = jnp.exp(cum[:, :, -1:, :] - cum) * dt_pages
    page_end = jnp.einsum("mksh,mkshp,mksn->mkhpn", tail, x_pages, b_pages, precision=HIGH)
    page_decay = jnp.exp(cum[:, :, -1, :])
    summary = (
        jnp.zeros((1,), jnp.float32),
        jnp.ones((2, local_heads), jnp.float32),
        jnp.zeros((2, local_heads, HEADDIM, STATE), jnp.float32),
    )
    for page in range(num_pages):
        summary = link_states(
            summary, (page_flags[page : page + 1], page_decay[:, page], page_end[:, page])
        )
    gate_through = summary[1] * (1.0 - summary[0])
    lane = jnp.arange(STATE)[None, None, None, :] == 0
    packed = jnp.concatenate(
        [summary[2], jnp.where(lane, gate_through[..., None, None], 0.0)], axis=2
    )
    vocab_local = lm_head.shape[1]
    half = vocab_local // 2
    feat = lm_head.shape[2]
    staged = [
        torus_gather(part, "dp", 4, n_dp // 4, row_first)
        for row_first, part in ((False, lm_head[:, :half]), (True, lm_head[:, half:]))
    ]
    firsts, packed = lax.optimization_barrier(([s[0] for s in staged], packed))
    every = lax.all_gather(packed, "dp")
    ends = every[:, :, :, :HEADDIM, :]
    through = every[:, :, :, HEADDIM, 0]
    peers = jnp.arange(n_dp)
    factor = jnp.where((peers < dp_index)[:, None, None], through, 1.0)
    weight = jnp.flip(jnp.cumprod(jnp.flip(factor, 0), axis=0), 0)
    weight = jnp.concatenate([weight[1:], jnp.ones_like(weight[:1])], axis=0)
    weight = jnp.where((peers < dp_index)[:, None, None], weight, 0.0)
    carried = jnp.sum(weight[..., None, None] * ends, axis=0)
    state_in = (1.0 - page_flags[0]) * carried
    outputs = []
    for page in range(num_pages):
        if page > 0:
            state_in = (1.0 - page_flags[page]) * (
                page_decay[:, page - 1][..., None, None] * state_in + page_end[:, page - 1]
            )
        y_carry = jnp.exp(cum[:, page])[..., None] * jnp.einsum(
            "mln,mhpn->mlhp", c_pages[:, page], state_in, precision=HIGH
        )
        outputs.append(y_intra[:, page] + y_carry + d_skip[:, None, :, None] * x_pages[:, page])
    scanned = jnp.stack(outputs, axis=1).reshape(2, tokens, local_inner)
    gated = scanned * jax.nn.silu(gate.astype(jnp.float32))
    gate_squares = jnp.sum(gated * gated, axis=2)
    unscaled = (gated * gate_gain[:, None, :]).astype(jnp.bfloat16)
    partial_out = jnp.einsum("mti,mid->mtd", unscaled, w_out, preferred_element_type=jnp.float32)
    extra = jnp.where(
        jnp.arange(128)[None, None, :] == 0, gate_squares[..., None], 0.0
    )
    summed = lax.psum_scatter(
        jnp.concatenate([partial_out, extra], axis=2), "mp", scatter_dimension=1, tiled=True
    )
    rows_here = summed.shape[1]
    gate_total = summed[:, :, D]
    mixed = summed[:, :, :D] * lax.rsqrt(gate_total[..., None] / INNER + EPS)
    mine = lax.dynamic_slice_in_dim(wide_in, mp_index * rows_here, rows_here, axis=1)
    final_part = rms_scale(mine + mixed, final_gain[:, None, :]).astype(jnp.bfloat16)
    seconds = [s[1](f) for s, f in zip(staged, firsts)]
    seconds, final_part = lax.optimization_barrier((seconds, final_part))
    seconds = [jnp.stack(moved).reshape((-1,) + moved[0].shape[1:]) for moved in seconds]
    grid_rows, grid_cols = (4, n_dp // 4)
    final_part = jnp.take(
        final_part.reshape(2, rows_here, n_dp, feat), jnp.stack(staged[0][2]), axis=2
    ).reshape(final_part.shape)
    final = lax.all_gather(final_part, "mp", axis=1, tiled=True)
    by_rows = final.reshape(2, tokens, grid_rows, grid_cols, feat)
    logits = jnp.concatenate(
        [
            jnp.einsum("mtabd,abmvd->mtv", by_rows,
                       seconds[0].reshape((grid_rows, grid_cols) + seconds[0].shape[1:]),
                       preferred_element_type=jnp.float32),
            jnp.einsum("mtabd,bamvd->mtv", by_rows,
                       seconds[1].reshape((grid_cols, grid_rows) + seconds[1].shape[1:]),
                       preferred_element_type=jnp.float32),
        ],
        axis=2,
    )
    top_here = jnp.max(logits, axis=2)
    exp_here = jnp.sum(jnp.exp(logits - top_here[..., None]), axis=2)
    local_ids = targets - mp_index * vocab_local
    hit = jnp.arange(vocab_local, dtype=jnp.int32)[None, None, :] == local_ids[None, :, None]
    picked_here = jnp.sum(jnp.where(hit, logits, 0.0), axis=2)
    stats = lax.all_gather(jnp.stack([top_here, exp_here, picked_here]), "mp")
    top = jnp.max(stats[:, 0], axis=0)
    exp_total = jnp.sum(stats[:, 1] * jnp.exp(stats[:, 0] - top[None]), axis=0)
    picked = jnp.sum(stats[:, 2], axis=0)
    logprob = picked - (top + jnp.log(exp_total))
    token_ratio = logprob[0] - logprob[1]
    request_count = owners.shape[0]
    page_sums = jnp.sum(token_ratio.reshape(num_pages, PAGE), axis=1)
    request_ids = jnp.arange(request_count, dtype=jnp.int32)
    all_onehot = (page_request[:, None] == request_ids[None, :]).astype(jnp.float32)
    counts = jnp.sum(all_onehot, axis=0) * PAGE
    my_onehot = (my_req[:, None] == request_ids[None, :]).astype(jnp.float32)
    seq_mean = jnp.sum(page_sums[:, None] * my_onehot, axis=0) / counts
    if n_dp & (n_dp - 1) == 0:
        bit = 1
        while bit < n_dp:
            seq_mean = seq_mean + lax.ppermute(seq_mean, "dp", [(i, i ^ bit) for i in range(n_dp)])
            bit *= 2
    else:
        seq_mean = lax.psum(seq_mean, "dp")
    owned = jnp.where(owners == dp_index, seq_mean, jnp.float32(0.0))[None, :]
    return (token_ratio, owned)


def solution(mesh):
    placed = (
        P(None, "dp", "mp"),
        P(),
        P(None, None, None, "mp"),
        P(),
        P(None, None, "mp"),
        P(None, None, "mp"),
        P(),
        P(None, "mp"),
        P(None, "mp"),
        P(None, "mp"),
        P(None, "mp"),
        P(None, "mp", None),
        P(),
        P(None, "mp", "dp"),
        P(),
        P("dp"),
        P(),
    )
    return jax.shard_map(
        local, mesh=mesh, in_specs=placed, out_specs=(P("dp"), P("dp", None)), check_vma=False
    )
```

```python
import jax
import jax.numpy as jnp
from jax import lax
from jax.sharding import PartitionSpec as P

D = 2048
INNER = 4096
HEADDIM = 64
STATE = 128
PAGE = 256


EPS = 1e-05
HIGH = lax.Precision.HIGHEST


def shifted(block, axis, distance):
    devices = range(lax.axis_size(axis))
    route = [(i - distance, i) for i in devices if i - distance in devices]
    return lax.ppermute(block, axis, route)


def entering(shard, axis, combine, identity):
    peers, index = (lax.axis_size(axis), lax.axis_index(axis))
    everything = jax.tree.map(lambda part: lax.all_gather(part, axis), shard)
    start = jax.tree.map(
        lambda part, zero: jnp.broadcast_to(jnp.asarray(zero, part.dtype), part.shape),
        shard,
        identity,
    )

    def turn(k, before):
        reached = k < index
        new = combine(before, jax.tree.map(lambda part: part[k], everything))
        return jax.tree.map(lambda a, b: jnp.where(reached, a, b), new, before)

    return lax.fori_loop(0, peers, turn, start)


def torus_gather(shard, axis, rows, cols, row_first):
    index = lax.axis_index(axis)
    row, col = (index // cols, index % cols)

    def step(block, along_rows, shifts, stacked=True):
        moved = [block]
        for s in shifts:
            if along_rows:
                route = [(r * cols + c, ((r + s) % rows) * cols + c) for r in range(rows) for c in range(cols)]
            else:
                route = [(r * cols + c, r * cols + (c + s) % cols) for r in range(rows) for c in range(cols)]
            moved.append(lax.ppermute(block, axis, route))
        return jnp.stack(moved) if stacked else moved

    if row_first:
        sources = [((row - a) % rows) * cols + (col - b) % cols for b in range(cols) for a in range(rows)]
    else:
        sources = [((row - a) % rows) * cols + (col - b) % cols for a in range(rows) for b in range(cols)]

    def second(first):
        return step(first, not row_first, range(1, cols if row_first else rows), stacked=False)

    return step(shard, row_first, range(1, rows if row_first else cols)), second, sources


def rms_scale(rows, gain):
    mean_square = jnp.mean(rows * rows, axis=-1, keepdims=True)
    return rows * lax.rsqrt(mean_square + EPS) * gain


def page_conv(current, previous, weights):
    width = weights.shape[1]
    length = current.shape[2]
    padded = jnp.concatenate([previous, current], axis=2).astype(jnp.float32)
    total = padded[:, :, width - 1 : width - 1 + length, :] * weights[:, None, None, width - 1, :]
    for back in range(1, width):
        begin = width - 1 - back
        total = (
            total
            + padded[:, :, begin : begin + length, :] * weights[:, None, None, width - 1 - back, :]
        )
    return jax.nn.silu(total).astype(jnp.bfloat16)


def link_states(earlier, later):
    later_flag = later[0]
    keep = 1.0 - later_flag
    return (
        jnp.maximum(earlier[0], later_flag),
        later[1] * (later_flag + keep * earlier[1]),
        later[2] + keep * later[1][..., None, None] * earlier[2],
    )


def local(
    hidden_in,
    in_gain,
    w_zx,
    w_bc,
    w_dt,
    conv_x,
    conv_bc,
    dt_bias,
    a_rate,
    d_skip,
    gate_gain,
    w_out,
    final_gain,
    lm_head,
    page_request,
    targets,
    owners,
):
    n_dp = lax.axis_size("dp")
    dp_index = lax.axis_index("dp")
    mp_index = lax.axis_index("mp")
    tokens = hidden_in.shape[1]
    num_pages = tokens // PAGE
    local_inner = w_zx.shape[3]
    local_heads = w_dt.shape[2]
    width = conv_x.shape[1]
    all_starts = page_request != jnp.concatenate([jnp.full((1,), -1, jnp.int32), page_request[:-1]])
    my_starts = lax.dynamic_slice_in_dim(all_starts, dp_index * num_pages, num_pages)
    my_req = lax.dynamic_slice_in_dim(page_request, dp_index * num_pages, num_pages)
    page_flags = my_starts.astype(jnp.float32)
    full_in = lax.all_gather(hidden_in, "mp", axis=2, tiled=True)
    wide_in = full_in.astype(jnp.float32)
    normed = rms_scale(wide_in, in_gain[:, None, :]).astype(jnp.bfloat16)
    zx_cols = w_zx.reshape(2, D, 2 * local_inner)
    proj_zx = jnp.einsum(
        "mtd,mde->mte", normed, zx_cols, preferred_element_type=jnp.float32
    ).astype(jnp.bfloat16)
    gate = proj_zx[:, :, :local_inner]
    values = proj_zx[:, :, local_inner:]
    proj_bc = jnp.einsum("mtd,mde->mte", normed, w_bc, preferred_element_type=jnp.float32).astype(
        jnp.bfloat16
    )
    proj_dt = jnp.einsum("mtd,mde->mte", normed, w_dt, preferred_element_type=jnp.float32).astype(
        jnp.bfloat16
    )
    rim_x, rim_bc = shifted(
        (values[:, tokens - (width - 1) :, :], proj_bc[:, tokens - (width - 1) :, :]), "dp", 1
    )
    value_pages = values.reshape(2, num_pages, PAGE, local_inner)
    bc_pages = proj_bc.reshape(2, num_pages, PAGE, 2 * STATE)
    cut_mask = my_starts[None, :, None, None]
    prev_x = jnp.concatenate([rim_x[:, None], value_pages[:, :-1, PAGE - (width - 1) :, :]], axis=1)
    prev_x = jnp.where(cut_mask, jnp.zeros_like(prev_x), prev_x)
    prev_bc = jnp.concatenate([rim_bc[:, None], bc_pages[:, :-1, PAGE - (width - 1) :, :]], axis=1)
    prev_bc = jnp.where(cut_mask, jnp.zeros_like(prev_bc), prev_bc)
    conv_values = page_conv(value_pages, prev_x, conv_x)
    conv_b_c = page_conv(bc_pages, prev_bc, conv_bc)
    step_size = jax.nn.softplus(proj_dt.astype(jnp.float32) + dt_bias[:, None, :])
    log_decay = -step_size * a_rate[:, None, :]
    x_pages = conv_values.astype(jnp.float32).reshape(2, num_pages, PAGE, local_heads, HEADDIM)
    b_pages = conv_b_c[..., :STATE].astype(jnp.float32)
    c_pages = conv_b_c[..., STATE:].astype(jnp.float32)
    dt_pages = step_size.reshape(2, num_pages, PAGE, local_heads)
    cum = jnp.cumsum(log_decay.reshape(2, num_pages, PAGE, local_heads), axis=2)
    inner = jnp.einsum("mkln,mksn->mkls", c_pages, b_pages, precision=HIGH)
    rows = jnp.arange(PAGE)
    lower = (rows[:, None] >= rows[None, :])[None, None, :, :, None]
    spread = cum[:, :, :, None, :] - cum[:, :, None, :, :]
    decay = jnp.where(lower, jnp.exp(jnp.where(lower, spread, 0.0)), 0.0)
    mixing = inner[..., None] * decay * dt_pages[:, :, None, :, :]
    y_intra = jnp.einsum("mklsh,mkshp->mklhp", mixing, x_pages, precision=HIGH)
    tail = jnp.exp(cum[:, :, -1:, :] - cum) * dt_pages
    page_end = jnp.einsum("mksh,mkshp,mksn->mkhpn", tail, x_pages, b_pages, precision=HIGH)
    page_decay = jnp.exp(cum[:, :, -1, :])
    summary = (
        jnp.zeros((1,), jnp.float32),
        jnp.ones((2, local_heads), jnp.float32),
        jnp.zeros((2, local_heads, HEADDIM, STATE), jnp.float32),
    )
    for page in range(num_pages):
        summary = link_states(
            summary, (page_flags[page : page + 1], page_decay[:, page], page_end[:, page])
        )
    gate_through = summary[1] * (1.0 - summary[0])
    lane = jnp.arange(STATE)[None, None, None, :] == 0
    packed = jnp.concatenate(
        [summary[2], jnp.where(lane, gate_through[..., None, None], 0.0)], axis=2
    )
    vocab_local = lm_head.shape[1]
    half = vocab_local // 2
    feat = lm_head.shape[2]
    staged = [
        torus_gather(part, "dp", 4, n_dp // 4, row_first)
        for row_first, part in ((False, lm_head[:, :half]), (True, lm_head[:, half:]))
    ]
    firsts, packed = lax.optimization_barrier(([s[0] for s in staged], packed))
    every = lax.all_gather(packed, "dp")
    ends = every[:, :, :, :HEADDIM, :]
    through = every[:, :, :, HEADDIM, 0]
    peers = jnp.arange(n_dp)
    factor = jnp.where((peers < dp_index)[:, None, None], through, 1.0)
    weight = jnp.flip(jnp.cumprod(jnp.flip(factor, 0), axis=0), 0)
    weight = jnp.concatenate([weight[1:], jnp.ones_like(weight[:1])], axis=0)
    weight = jnp.where((peers < dp_index)[:, None, None], weight, 0.0)
    carried = jnp.sum(weight[..., None, None] * ends, axis=0)
    state_in = (1.0 - page_flags[0]) * carried
    outputs = []
    for page in range(num_pages):
        if page > 0:
            state_in = (1.0 - page_flags[page]) * (
                page_decay[:, page - 1][..., None, None] * state_in + page_end[:, page - 1]
            )
        y_carry = jnp.exp(cum[:, page])[..., None] * jnp.einsum(
            "mln,mhpn->mlhp", c_pages[:, page], state_in, precision=HIGH
        )
        outputs.append(y_intra[:, page] + y_carry + d_skip[:, None, :, None] * x_pages[:, page])
    scanned = jnp.stack(outputs, axis=1).reshape(2, tokens, local_inner)
    gated = scanned * jax.nn.silu(gate.astype(jnp.float32))
    gate_squares = jnp.sum(gated * gated, axis=2)
    unscaled = (gated * gate_gain[:, None, :]).astype(jnp.bfloat16)
    partial_out = jnp.einsum("mti,mid->mtd", unscaled, w_out, preferred_element_type=jnp.float32)
    extra = jnp.where(
        jnp.arange(128)[None, None, :] == 0, gate_squares[..., None], 0.0
    )
    summed = lax.psum_scatter(
        jnp.concatenate([partial_out, extra], axis=2), "mp", scatter_dimension=1, tiled=True
    )
    rows_here = summed.shape[1]
    gate_total = summed[:, :, D]
    mixed = summed[:, :, :D] * lax.rsqrt(gate_total[..., None] / INNER + EPS)
    mine = lax.dynamic_slice_in_dim(wide_in, mp_index * rows_here, rows_here, axis=1)
    final_part = rms_scale(mine + mixed, final_gain[:, None, :]).astype(jnp.bfloat16)
    seconds = [s[1](f) for s, f in zip(staged, firsts)]
    seconds, final_part = lax.optimization_barrier((seconds, final_part))
    seconds = [jnp.stack(moved).reshape((-1,) + moved[0].shape[1:]) for moved in seconds]
    grid_rows, grid_cols = (4, n_dp // 4)
    final_part = jnp.take(
        final_part.reshape(2, rows_here, n_dp, feat), jnp.stack(staged[0][2]), axis=2
    ).reshape(final_part.shape)
    final = lax.all_gather(final_part, "mp", axis=1, tiled=True)
    by_rows = final.reshape(2, tokens, grid_rows, grid_cols, feat)
    logits = jnp.concatenate(
        [
            jnp.einsum("mtabd,abmvd->mtv", by_rows,
                       seconds[0].reshape((grid_rows, grid_cols) + seconds[0].shape[1:]),
                       preferred_element_type=jnp.float32),
            jnp.einsum("mtabd,bamvd->mtv", by_rows,
                       seconds[1].reshape((grid_cols, grid_rows) + seconds[1].shape[1:]),
                       preferred_element_type=jnp.float32),
        ],
        axis=2,
    )
    top_here = jnp.max(logits, axis=2)
    exp_here = jnp.sum(jnp.exp(logits - top_here[..., None]), axis=2)
    local_ids = targets - mp_index * vocab_local
    hit = jnp.arange(vocab_local, dtype=jnp.int32)[None, None, :] == local_ids[None, :, None]
    picked_here = jnp.sum(jnp.where(hit, logits, 0.0), axis=2)
    stats = lax.all_gather(jnp.stack([top_here, exp_here, picked_here]), "mp")
    top = jnp.max(stats[:, 0], axis=0)
    exp_total = jnp.sum(stats[:, 1] * jnp.exp(stats[:, 0] - top[None]), axis=0)
    picked = jnp.sum(stats[:, 2], axis=0)
    logprob = picked - (top + jnp.log(exp_total))
    token_ratio = logprob[0] - logprob[1]
    request_count = owners.shape[0]
    page_sums = jnp.sum(token_ratio.reshape(num_pages, PAGE), axis=1)
    request_ids = jnp.arange(request_count, dtype=jnp.int32)
    all_onehot = (page_request[:, None] == request_ids[None, :]).astype(jnp.float32)
    counts = jnp.sum(all_onehot, axis=0) * PAGE
    my_onehot = (my_req[:, None] == request_ids[None, :]).astype(jnp.float32)
    seq_mean = jnp.sum(page_sums[:, None] * my_onehot, axis=0) / counts
    if n_dp % 4 == 0:
        grid_cols = n_dp // 4
        for ring, stride in ((grid_cols, 1), (4, grid_cols)):
            moved = []
            for shift in range(1, ring):
                route = [
                    (i, (i // (ring * stride)) * ring * stride + (i + shift * stride) % (ring * stride))
                    for i in range(n_dp)
                ]
                moved.append(lax.ppermute(seq_mean, "dp", route))
            seq_mean = sum(moved, seq_mean)
    elif n_dp & (n_dp - 1) == 0:
        bit = 1
        while bit < n_dp:
            seq_mean = seq_mean + lax.ppermute(seq_mean, "dp", [(i, i ^ bit) for i in range(n_dp)])
            bit *= 2
    else:
        seq_mean = lax.psum(seq_mean, "dp")
    owned = jnp.where(owners == dp_index, seq_mean, jnp.float32(0.0))[None, :]
    return (token_ratio, owned)


def solution(mesh):
    placed = (
        P(None, "dp", "mp"),
        P(),
        P(None, None, None, "mp"),
        P(),
        P(None, None, "mp"),
        P(None, None, "mp"),
        P(),
        P(None, "mp"),
        P(None, "mp"),
        P(None, "mp"),
        P(None, "mp"),
        P(None, "mp", None),
        P(),
        P(None, "mp", "dp"),
        P(),
        P("dp"),
        P(),
    )
    return jax.shard_map(
        local, mesh=mesh, in_specs=placed, out_specs=(P("dp"), P("dp", None)), check_vma=False
    )
```
